128 devices in a mesh: shard: 32 (over x, y, core), tensor: 4 (over z).
Axes of the slice: x: 4, y: 4, z: 4, core: 2. Of those that a mesh axis runs over, the one named last changes fastest.
Arguments:
- grads: bfloat16 [384, 256, 256], P('shard', 'tensor'), may hold values from -60 to 60
- owner: int32 [384], replicated, may hold values from 0 to 31, as said below
- slot: int32 [384], replicated, may hold values from 0 to 23, as said below
- stat_left: float32 [768, 256, 256], P('shard', 'tensor'), may hold values from -144 to 2704, as said below
- stat_right: float32 [768, 256, 256], P('shard', 'tensor'), may hold values from -144 to 2704, as said below
- root_left: float32 [768, 256, 256], P('shard', 'tensor'), may hold values from -0.72 to 2.72, as said below
- root_right: float32 [768, 256, 256], P('shard'), may hold values from -0.72 to 2.72, as said below
- moment: float32 [768, 256, 256], P('shard', 'tensor'), may hold values from 0.1 to 10
- momentum: float32 [768, 256, 256], P('shard', 'tensor'), may hold values from -6 to 6
- master: float32 [768, 256, 256], P('shard', 'tensor'), may hold values from -0.3 to 0.3
Outputs:
- stat_left_new: float32 [768, 256, 256], P('shard', 'tensor')
- stat_right_new: float32 [768, 256, 256], P('shard', 'tensor')
- moment_new: float32 [768, 256, 256], P('shard', 'tensor')
- momentum_new: float32 [768, 256, 256], P('shard', 'tensor')
- master_new: float32 [768, 256, 256], P('shard', 'tensor')
- weights_new: bfloat16 [384, 256, 256], P('shard', 'tensor')
The draws below stay inside these ranges and needn't reach their ends.
Inputs may be any that keep to these rules, and one draw needn't show every extreme that they name: Each owner group holds at most 24 blocks, some exactly 24; no owner group holds two blocks of one shard group (blocks b with equal b // 12). `slot`: the blocks of one owner group have distinct slots. `stat_left`: Symmetric. `stat_right`: Symmetric. `root_left`: Symmetric. `root_right`: Symmetric.
All inputs are finite; a program needn't handle non-finite values.
Results may differ from the reference program's by a relative error of at most 0.001.
Values may be sent and summed in bfloat16 or wider, within the bound.
No kernel may reach another device: no remote copies, remote signals or barrier semaphores. Data moves between devices by JAX's collectives and lax.ppermute only.
A program may use at most 128 MiB of HBM per device.

```python
import math
import jax
import jax.numpy as jnp
from jax import lax

BLK = 256
GROUPS = 32
NB_SH = 12
CAP = 24
NBLK = 384


def deal(key):
    key_list = jax.random.split(jax.random.fold_in(key, 11), 5)
    pair_count = GROUPS // 2
    spread = jax.random.randint(key_list[0], (pair_count,), 0, NB_SH + 1).astype(jnp.int32)
    spread = spread.at[0].set(NB_SH)
    loads = jnp.stack([NB_SH + spread, NB_SH - spread], axis=1).reshape(GROUPS).astype(jnp.int32)
    run_ends = jnp.cumsum(loads).astype(jnp.int32)
    run_starts = run_ends - loads
    total = NB_SH * GROUPS
    position = jnp.arange(total, dtype=jnp.int32)
    run_index = jnp.sum((run_ends[None, :] <= position[:, None]).astype(jnp.int32), axis=1).astype(jnp.int32)
    within = position - run_starts[run_index]
    owner_perm = jax.random.permutation(key_list[1], GROUPS).astype(jnp.int32)
    owner_id = owner_perm[run_index]
    slot_shift = jax.random.randint(key_list[2], (GROUPS,), 0, CAP).astype(jnp.int32)
    slot_value = (within + slot_shift[owner_id]) % CAP
    group_perm = jax.random.permutation(key_list[3], GROUPS).astype(jnp.int32)
    group_id = group_perm[position % GROUPS]
    rank_shift = jax.random.randint(key_list[4], (GROUPS,), 0, NB_SH).astype(jnp.int32)
    rank_value = (position // GROUPS + rank_shift[group_id]) % NB_SH
    block_id = group_id * NB_SH + rank_value
    owners = jnp.zeros((total,), jnp.int32).at[block_id].set(owner_id)
    slots = jnp.zeros((total,), jnp.int32).at[block_id].set(slot_value)
    return (owners, slots)


def draw_owner(key, part):
    return deal(key)[0]


def draw_slot(key, part):
    return deal(key)[1]


def draw_grads(key, part):
    key_list = jax.random.split(jax.random.fold_in(key, 23), 3)
    row_scale = jnp.exp(jax.random.uniform(key_list[1], (NBLK, BLK, 1), minval=-1.15, maxval=1.15))
    col_scale = jnp.exp(jax.random.uniform(key_list[2], (NBLK, 1, BLK), minval=-1.15, maxval=1.15))
    basis = jnp.clip(jax.random.normal(key_list[0], (NBLK, BLK, BLK)), -6.0, 6.0)
    return (basis * row_scale * col_scale).astype(jnp.bfloat16)


def sym_field(key, diag_lo, diag_hi, off_scale):
    key_list = jax.random.split(key, 2)
    basis = jnp.clip(jax.random.normal(key_list[0], (GROUPS * CAP, BLK, BLK)), -6.0, 6.0)
    symmetric = (basis + jnp.swapaxes(basis, 1, 2)) * off_scale
    diagonal = jnp.exp(jax.random.uniform(key_list[1], (GROUPS * CAP, BLK, 1), minval=math.log(diag_lo), maxval=math.log(diag_hi)))
    identity_mat = jnp.eye(BLK, dtype=jnp.float32)[None]
    return (symmetric * (1.0 - identity_mat) + identity_mat * diagonal).astype(jnp.float32)


def draw_stat_left(key, part):
    return sym_field(jax.random.fold_in(key, 31), 0.25 * BLK, 10.0 * BLK, 8.0)


def draw_stat_right(key, part):
    return sym_field(jax.random.fold_in(key, 37), 0.25 * BLK, 10.0 * BLK, 8.0)


def draw_root_left(key, part):
    return sym_field(jax.random.fold_in(key, 41), 0.5, 2.0, 0.04)


def draw_root_right(key, part):
    return sym_field(jax.random.fold_in(key, 43), 0.5, 2.0, 0.04)


def steps_of(rng, dims, pieces, low, high):
    level = 1.0
    for dim, parts in pieces:
        heights = jax.random.uniform(jax.random.fold_in(jax.random.fold_in(rng, 6), dim), (parts,), jnp.float32, low / len(pieces), high / len(pieces))
        level = level * jnp.repeat(jnp.exp(heights), dims[dim] // parts).reshape((-1,) + (1,) * (len(dims) - 1 - dim))
    return level


def centred(own_key, extent, scale, reach, shards=(), held_as=jnp.bfloat16):
    values = scale * jax.random.normal(own_key, extent, jnp.float32)
    if shards:
        values = values * steps_of(own_key, extent, shards, -0.22, 0.18)
    return jnp.clip(values, -reach, reach).astype(held_as)


def setup_inputs(seed: int = 0) -> dict:
    keys = jax.random.split(jax.random.key(seed), 11)
    grads = draw_grads(jax.random.fold_in(keys[10], 71), 0)
    owner = draw_owner(jax.random.fold_in(keys[10], 71), 0)
    slot = draw_slot(jax.random.fold_in(keys[10], 71), 0)
    stat_left = draw_stat_left(jax.random.fold_in(keys[10], 71), 0)
    stat_right = draw_stat_right(jax.random.fold_in(keys[10], 71), 0)
    root_left = draw_root_left(jax.random.fold_in(keys[10], 71), 0)
    root_right = draw_root_right(jax.random.fold_in(keys[10], 71), 0)
    moment = jnp.clip(jnp.exp(math.log(10.0) - 4.6051702 * jax.random.uniform(keys[7], (GROUPS * CAP, BLK, BLK), jnp.float32) ** steps_of(keys[7], (GROUPS * CAP, BLK, BLK), ((0, 32), (1, 4)), -0.2, 0.2)), 0.1, 10.0)
    momentum = centred(keys[8], (GROUPS * CAP, BLK, BLK), 1.0, 6.0, ((0, 32), (1, 4)), jnp.float32)
    master = centred(keys[9], (GROUPS * CAP, BLK, BLK), 0.05, 0.3, ((0, 32), (1, 4)), jnp.float32)
    return dict(grads=grads, owner=owner, slot=slot, stat_left=stat_left, stat_right=stat_right, root_left=root_left, root_right=root_right, moment=moment, momentum=momentum, master=master)


beta_stat = 0.95
beta_mom = 0.9
learn_rate = 0.01
eps_root = 1e-08
eps_mean = 1e-06

def one_slot(items):
    grad_block, left_stat, right_stat, root_one, root_two, second, velocity, weight = items
    highest = lax.Precision.HIGHEST
    grad_full = grad_block.astype(jnp.float32)
    left_new = beta_stat * left_stat + (1.0 - beta_stat) * jnp.dot(grad_full, grad_full.T, preferred_element_type=jnp.float32, precision=highest)
    right_new = beta_stat * right_stat + (1.0 - beta_stat) * jnp.dot(grad_full.T, grad_full, preferred_element_type=jnp.float32, precision=highest)
    second_new = beta_stat * second + (1.0 - beta_stat) * grad_full * grad_full
    adam_step = grad_full / (jnp.sqrt(second_new) + eps_root)
    precond = jnp.dot(root_one, grad_full, preferred_element_type=jnp.float32, precision=highest)
    precond = jnp.dot(precond, root_two, preferred_element_type=jnp.float32, precision=highest)
    scale_ratio = jnp.sqrt(jnp.mean(adam_step * adam_step) + eps_mean) / jnp.sqrt(jnp.mean(precond * precond) + eps_mean)
    velocity_new = beta_mom * velocity + (1.0 - beta_mom) * scale_ratio * precond
    weight_new = weight - learn_rate * velocity_new
    return (left_new, right_new, second_new, velocity_new, weight_new)

def reference(grads, owner, slot, stat_left, stat_right, root_left, root_right, moment, momentum, master):
    targets = (owner * CAP + slot).astype(jnp.int32)
    grad_slots = jnp.zeros((GROUPS * CAP, BLK, BLK), jnp.bfloat16).at[targets].set(grads)
    left_new, right_new, second_new, velocity_new, weight_new = lax.map(one_slot, (grad_slots, stat_left, stat_right, root_left, root_right, moment, momentum, master))
    weights_new = weight_new[targets].astype(jnp.bfloat16)
    return (left_new, right_new, second_new, velocity_new, weight_new, weights_new)
```

```python
import jax
import jax.numpy as jnp
from jax import lax
from jax.sharding import PartitionSpec as P

beta_stat = 0.95
beta_mom = 0.9
learn_rate = 0.01
eps_root = 1e-08
eps_mean = 1e-06


def split3(x):
    hi = x.astype(jnp.bfloat16)
    rest = x - hi.astype(jnp.float32)
    mid = rest.astype(jnp.bfloat16)
    lo = (rest - mid.astype(jnp.float32)).astype(jnp.bfloat16)
    return hi, mid, lo


def gather_rows(piece, splits, tensor_index):
    right = [(i, (i + 1) % splits) for i in range(splits)]
    left = [(i, (i - 1) % splits) for i in range(splits)]
    from_left = lax.ppermute(piece, "tensor", right)
    from_right = lax.ppermute(piece, "tensor", left)
    half = piece.shape[0] // 2
    far_a = lax.ppermute(from_left[:half], "tensor", right)
    far_b = lax.ppermute(from_right[half:], "tensor", left)
    far = jnp.concatenate([far_a, far_b], 0)
    rows = piece.shape[1]
    whole = jnp.zeros((piece.shape[0], rows * splits, piece.shape[2]), piece.dtype)
    for shift, part in ((0, piece), (1, from_right), (2, far), (splits - 1, from_left)):
        start = ((tensor_index + shift) % splits) * rows
        whole = lax.dynamic_update_slice_in_dim(whole, part, start, 1)
    return whole


def on_device(
    grads, owner, slot, stat_left, stat_right, root_left, root_right, moment, momentum, master
):
    groups = lax.axis_size("shard")
    splits = lax.axis_size("tensor")
    slots_dev = stat_left.shape[0]
    rows_dev = stat_left.shape[1]
    order = stat_left.shape[2]
    blocks_group = grads.shape[0]
    shard_index = lax.axis_index("shard")
    tensor_index = lax.axis_index("tensor")
    owner_grid = owner.reshape(groups, blocks_group)
    slot_grid = slot.reshape(groups, blocks_group)
    local_owner = lax.dynamic_index_in_dim(owner_grid, shard_index, 0, keepdims=False)
    hit_mask = owner_grid == shard_index
    slot_ids = jnp.arange(slots_dev, dtype=jnp.int32)
    select = jnp.sum(
        (slot_grid[None, :, :] == slot_ids[:, None, None]) & hit_mask[None, :, :], axis=2
    ).astype(jnp.bfloat16)
    group_ids = jnp.arange(groups, dtype=jnp.int32)
    picker = (local_owner[None, :] == group_ids[:, None]).astype(jnp.bfloat16)
    row_start = tensor_index * rows_dev
    outgoing = jnp.einsum(
        "gi,ixy->gxy", picker, grads, preferred_element_type=jnp.float32
    ).astype(jnp.bfloat16)
    arrived = lax.all_to_all(outgoing, "shard", split_axis=0, concat_axis=0, tiled=True)
    grad_piece = jnp.einsum(
        "kg,gxy->kxy", select, arrived, preferred_element_type=jnp.float32
    ).astype(jnp.bfloat16)
    grad_whole = gather_rows(grad_piece, splits, tensor_index)
    highest = lax.Precision.HIGHEST
    f32 = jnp.float32
    grad_cols = lax.dynamic_slice_in_dim(grad_whole, row_start, rows_dev, 2)
    left_new = beta_stat * stat_left + (1.0 - beta_stat) * jnp.einsum(
        "kij,klj->kil", grad_piece, grad_whole, preferred_element_type=f32
    )
    right_new = beta_stat * stat_right + (1.0 - beta_stat) * jnp.einsum(
        "kji,kjl->kil", grad_cols, grad_whole, preferred_element_type=f32
    )
    grad_rows = grad_piece.astype(f32)
    second_new = beta_stat * moment + (1.0 - beta_stat) * grad_rows * grad_rows
    adam_step = grad_rows / (jnp.sqrt(second_new) + eps_root)
    root_hi, root_mid, root_lo = split3(root_left)
    precond = (
        jnp.einsum("kij,kjl->kil", root_hi, grad_whole, preferred_element_type=f32)
        + jnp.einsum("kij,kjl->kil", root_mid, grad_whole, preferred_element_type=f32)
        + jnp.einsum("kij,kjl->kil", root_lo, grad_whole, preferred_element_type=f32)
    )
    precond = jnp.einsum("kij,kjl->kil", precond, root_right, precision=highest)
    adam_sum, precond_sum = lax.psum(
        (jnp.sum(adam_step * adam_step, axis=(1, 2)), jnp.sum(precond * precond, axis=(1, 2))),
        "tensor",
    )
    entries = float(rows_dev * splits * order)
    scale_ratio = jnp.sqrt(adam_sum / entries + eps_mean) / jnp.sqrt(
        precond_sum / entries + eps_mean
    )
    velocity_new = beta_mom * momentum + (1.0 - beta_mom) * scale_ratio[:, None, None] * precond
    weight_new = master - learn_rate * velocity_new
    weight_half = weight_new.astype(jnp.bfloat16)
    returning = jnp.einsum(
        "kg,kxy->gxy", select, weight_half, preferred_element_type=jnp.float32
    ).astype(jnp.bfloat16)
    back_rows = lax.all_to_all(returning, "shard", split_axis=0, concat_axis=0, tiled=True)
    weights_local = jnp.take(back_rows, local_owner, axis=0)
    return (left_new, right_new, second_new, velocity_new, weight_new, weights_local)


def solution(mesh):
    placed = (
        P("shard", "tensor", None),
        P(),
        P(),
        P("shard", "tensor", None),
        P("shard", "tensor", None),
        P("shard", "tensor", None),
        P("shard", None, None),
        P("shard", "tensor", None),
        P("shard", "tensor", None),
        P("shard", "tensor", None),
    )
    return jax.shard_map(
        on_device,
        mesh=mesh,
        in_specs=placed,
        out_specs=(
            P("shard", "tensor", None),
            P("shard", "tensor", None),
            P("shard", "tensor", None),
            P("shard", "tensor", None),
            P("shard", "tensor", None),
            P("shard", "tensor", None),
        ),
        check_vma=False,
    )
```

```python
import jax
import jax.numpy as jnp
from jax import lax
from jax.sharding import PartitionSpec as P

beta_stat = 0.95
beta_mom = 0.9
learn_rate = 0.01
eps_root = 1e-08
eps_mean = 1e-06


def gather_rows(piece, splits, tensor_index):
    right = [(i, (i + 1) % splits) for i in range(splits)]
    left = [(i, (i - 1) % splits) for i in range(splits)]
    from_left = lax.ppermute(piece, "tensor", right)
    from_right = lax.ppermute(piece, "tensor", left)
    half = piece.shape[0] // 2
    far_a = lax.ppermute(from_left[:half], "tensor", right)
    far_b = lax.ppermute(from_right[half:], "tensor", left)
    far = jnp.concatenate([far_a, far_b], 0)
    by_shift = (piece, from_right, far, from_left)

    def ordered(first):
        return lambda: jnp.concatenate([by_shift[(p - first) % splits] for p in range(splits)], 1)

    return lax.switch(tensor_index, [ordered(first) for first in range(splits)])


def on_device(
    grads, owner, slot, stat_left, stat_right, root_left, root_right, moment, momentum, master
):
    groups = lax.axis_size("shard")
    splits = lax.axis_size("tensor")
    slots_dev = stat_left.shape[0]
    rows_dev = stat_left.shape[1]
    order = stat_left.shape[2]
    blocks_group = grads.shape[0]
    shard_index = lax.axis_index("shard")
    tensor_index = lax.axis_index("tensor")
    owner_grid = owner.reshape(groups, blocks_group)
    slot_grid = slot.reshape(groups, blocks_group)
    local_owner = lax.dynamic_index_in_dim(owner_grid, shard_index, 0, keepdims=False)
    hit_mask = owner_grid == shard_index
    slot_ids = jnp.arange(slots_dev, dtype=jnp.int32)
    select = jnp.sum(
        (slot_grid[None, :, :] == slot_ids[:, None, None]) & hit_mask[None, :, :], axis=2
    ).astype(jnp.bfloat16)
    group_ids = jnp.arange(groups, dtype=jnp.int32)
    picker = (local_owner[None, :] == group_ids[:, None]).astype(jnp.bfloat16)
    row_start = tensor_index * rows_dev
    outgoing = jnp.einsum(
        "gi,ixy->gxy", picker, grads, preferred_element_type=jnp.float32
    ).astype(jnp.bfloat16)
    arrived = lax.all_to_all(outgoing, "shard", split_axis=0, concat_axis=0, tiled=True)
    grad_piece = jnp.einsum(
        "kg,gxy->kxy", select, arrived, preferred_element_type=jnp.float32
    ).astype(jnp.bfloat16)
    grad_whole = gather_rows(grad_piece, splits, tensor_index)
    highest = lax.Precision.HIGHEST
    f32 = jnp.float32
    grad_cols = lax.dynamic_slice_in_dim(grad_whole, row_start, rows_dev, 2)
    left_new = beta_stat * stat_left + (1.0 - beta_stat) * jnp.einsum(
        "kij,klj->kil", grad_piece, grad_whole, preferred_element_type=f32
    )
    right_new = beta_stat * stat_right + (1.0 - beta_stat) * jnp.einsum(
        "kji,kjl->kil", grad_cols, grad_whole, preferred_element_type=f32
    )
    grad_rows = grad_piece.astype(f32)
    second_new = beta_stat * moment + (1.0 - beta_stat) * grad_rows * grad_rows
    adam_step = grad_rows / (jnp.sqrt(second_new) + eps_root)
    precond = jnp.einsum("kij,kjl->kil", root_left, grad_whole.astype(f32), precision=highest)
    precond = jnp.einsum("kij,kjl->kil", precond, root_right, precision=highest)
    sums = jnp.stack(
        [jnp.sum(adam_step * adam_step, axis=(1, 2)), jnp.sum(precond * precond, axis=(1, 2))]
    )
    step = 1
    while step < splits:
        sums = sums + lax.ppermute(sums, "tensor", [(i, i ^ step) for i in range(splits)])
        step *= 2
    adam_sum, precond_sum = sums[0], sums[1]
    entries = float(rows_dev * splits * order)
    scale_ratio = jnp.sqrt(adam_sum / entries + eps_mean) / jnp.sqrt(
        precond_sum / entries + eps_mean
    )
    velocity_new = beta_mom * momentum + (1.0 - beta_mom) * scale_ratio[:, None, None] * precond
    weight_new = master - learn_rate * velocity_new
    weight_half = weight_new.astype(jnp.bfloat16)
    returning = jnp.einsum(
        "kg,kxy->gxy", select, weight_half, preferred_element_type=jnp.float32
    ).astype(jnp.bfloat16)
    back_rows = lax.all_to_all(returning, "shard", split_axis=0, concat_axis=0, tiled=True)
    weights_local = jnp.take(back_rows, local_owner, axis=0)
    return (left_new, right_new, second_new, velocity_new, weight_new, weights_local)


def solution(mesh):
    placed = (
        P("shard", "tensor", None),
        P(),
        P(),
        P("shard", "tensor", None),
        P("shard", "tensor", None),
        P("shard", "tensor", None),
        P("shard", None, None),
        P("shard", "tensor", None),
        P("shard", "tensor", None),
        P("shard", "tensor", None),
    )
    return jax.shard_map(
        on_device,
        mesh=mesh,
        in_specs=placed,
        out_specs=(
            P("shard", "tensor", None),
            P("shard", "tensor", None),
            P("shard", "tensor", None),
            P("shard", "tensor", None),
            P("shard", "tensor", None),
            P("shard", "tensor", None),
        ),
        check_vma=False,
    )
```

```python
import jax
import jax.numpy as jnp
from jax import lax
from jax.sharding import PartitionSpec as P

beta_stat = 0.95
beta_mom = 0.9
learn_rate = 0.01
eps_root = 1e-08
eps_mean = 1e-06


def gather_rows(first_half, second_half, splits, tensor_index):
    right = [(i, (i + 1) % splits) for i in range(splits)]
    left = [(i, (i - 1) % splits) for i in range(splits)]
    left_a = lax.ppermute(first_half, "tensor", right)
    right_b = lax.ppermute(second_half, "tensor", left)
    left_b = lax.ppermute(second_half, "tensor", right)
    right_a = lax.ppermute(first_half, "tensor", left)
    far_a = lax.ppermute(left_a, "tensor", right)
    far_b = lax.ppermute(right_b, "tensor", left)
    by_shift = (
        (first_half, second_half),
        (right_a, right_b),
        (far_a, far_b),
        (left_a, left_b),
    )

    def ordered(first):
        def build():
            rows = [jnp.concatenate(by_shift[(p - first) % splits], 0) for p in range(splits)]
            return jnp.concatenate(rows, 1)

        return build

    return lax.switch(tensor_index, [ordered(first) for first in range(splits)])


def pick(source, index, valid):
    taken = jnp.take(source, index, axis=0, mode="clip")
    return jnp.where(valid[:, None, None], taken, jnp.zeros((), source.dtype))


def on_device(
    grads, owner, slot, stat_left, stat_right, root_left, root_right, moment, momentum, master
):
    groups = lax.axis_size("shard")
    splits = lax.axis_size("tensor")
    slots_dev = stat_left.shape[0]
    rows_dev = stat_left.shape[1]
    order = stat_left.shape[2]
    blocks_group = grads.shape[0]
    shard_index = lax.axis_index("shard")
    tensor_index = lax.axis_index("tensor")
    owner_grid = owner.reshape(groups, blocks_group)
    slot_grid = slot.reshape(groups, blocks_group)
    local_owner = lax.dynamic_index_in_dim(owner_grid, shard_index, 0, keepdims=False)
    hit_mask = owner_grid == shard_index
    slot_ids = jnp.arange(slots_dev, dtype=jnp.int32)
    group_ids = jnp.arange(groups, dtype=jnp.int32)
    slot_match = jnp.any(
        (slot_grid[None, :, :] == slot_ids[:, None, None]) & hit_mask[None, :, :], axis=2
    )
    src_of_slot = jnp.argmax(slot_match, axis=1).astype(jnp.int32)
    slot_filled = jnp.any(slot_match, axis=1)
    slot_of_src = jnp.argmax(slot_match, axis=0).astype(jnp.int32)
    src_sent = jnp.any(slot_match, axis=0)
    dest_match = local_owner[None, :] == group_ids[:, None]
    block_of_dest = jnp.argmax(dest_match, axis=1).astype(jnp.int32)
    dest_used = jnp.any(dest_match, axis=1)
    row_start = tensor_index * rows_dev
    outgoing = pick(grads, block_of_dest, dest_used)
    arrived = lax.all_to_all(outgoing, "shard", split_axis=0, concat_axis=0, tiled=True)
    half = slots_dev // 2
    first_half = pick(arrived, src_of_slot[:half], slot_filled[:half])
    second_half = pick(arrived, src_of_slot[half:], slot_filled[half:])
    grad_piece = jnp.concatenate([first_half, second_half], 0)
    grad_whole = gather_rows(first_half, second_half, splits, tensor_index)
    highest = lax.Precision.HIGHEST
    f32 = jnp.float32
    grad_cols = lax.dynamic_slice_in_dim(grad_whole, row_start, rows_dev, 2)
    left_new = beta_stat * stat_left + (1.0 - beta_stat) * jnp.einsum(
        "kij,klj->kil", grad_piece, grad_whole, preferred_element_type=f32
    )
    right_new = beta_stat * stat_right + (1.0 - beta_stat) * jnp.einsum(
        "kji,kjl->kil", grad_cols, grad_whole, preferred_element_type=f32
    )
    grad_rows = grad_piece.astype(f32)
    second_new = beta_stat * moment + (1.0 - beta_stat) * grad_rows * grad_rows
    adam_step = grad_rows / (jnp.sqrt(second_new) + eps_root)
    precond = jnp.einsum("kij,kjl->kil", root_left, grad_whole.astype(f32), precision=highest)
    precond = jnp.einsum("kij,kjl->kil", precond, root_right, precision=highest)
    sums = jnp.stack(
        [jnp.sum(adam_step * adam_step, axis=(1, 2)), jnp.sum(precond * precond, axis=(1, 2))]
    )
    step = 1
    while step < splits:
        sums = sums + lax.ppermute(sums, "tensor", [(i, i ^ step) for i in range(splits)])
        step *= 2
    adam_sum, precond_sum = sums[0], sums[1]
    entries = float(rows_dev * splits * order)
    scale_ratio = jnp.sqrt(adam_sum / entries + eps_mean) / jnp.sqrt(
        precond_sum / entries + eps_mean
    )
    velocity_new = beta_mom * momentum + (1.0 - beta_mom) * scale_ratio[:, None, None] * precond
    weight_new = master - learn_rate * velocity_new
    weight_half = weight_new.astype(jnp.bfloat16)
    returning = pick(weight_half, slot_of_src, src_sent)
    back_rows = lax.all_to_all(returning, "shard", split_axis=0, concat_axis=0, tiled=True)
    weights_local = jnp.take(back_rows, local_owner, axis=0)
    return (left_new, right_new, second_new, velocity_new, weight_new, weights_local)


def solution(mesh):
    placed = (
        P("shard", "tensor", None),
        P(),
        P(),
        P("shard", "tensor", None),
        P("shard", "tensor", None),
        P("shard", "tensor", None),
        P("shard", None, None),
        P("shard", "tensor", None),
        P("shard", "tensor", None),
        P("shard", "tensor", None),
    )
    return jax.shard_map(
        on_device,
        mesh=mesh,
        in_specs=placed,
        out_specs=(
            P("shard", "tensor", None),
            P("shard", "tensor", None),
            P("shard", "tensor", None),
            P("shard", "tensor", None),
            P("shard", "tensor", None),
            P("shard", "tensor", None),
        ),
        check_vma=False,
    )
```

```python
import jax
import jax.numpy as jnp
from jax import lax
from jax.sharding import PartitionSpec as P

beta_stat = 0.95
beta_mom = 0.9
learn_rate = 0.01
eps_root = 1e-08
eps_mean = 1e-06


def gather_rows(first_half, second_half, splits, tensor_index):
    right = [(i, (i + 1) % splits) for i in range(splits)]
    left = [(i, (i - 1) % splits) for i in range(splits)]
    left_a = lax.ppermute(first_half, "tensor", right)
    right_b = lax.ppermute(second_half, "tensor", left)
    left_b = lax.ppermute(second_half, "tensor", right)
    right_a = lax.ppermute(first_half, "tensor", left)
    far_a = lax.ppermute(left_a, "tensor", right)
    far_b = lax.ppermute(right_b, "tensor", left)
    by_shift = (
        (first_half, second_half),
        (right_a, right_b),
        (far_a, far_b),
        (left_a, left_b),
    )

    def ordered(first):
        def build():
            rows = [jnp.concatenate(by_shift[(p - first) % splits], 0) for p in range(splits)]
            return jnp.concatenate(rows, 1)

        return build

    return lax.switch(tensor_index, [ordered(first) for first in range(splits)])


def pick(source, index, valid):
    taken = jnp.take(source, index, axis=0, mode="clip")
    return jnp.where(valid[:, None, None], taken, jnp.zeros((), source.dtype))


def on_device(
    grads, owner, slot, stat_left, stat_right, root_left, root_right, moment, momentum, master
):
    groups = lax.axis_size("shard")
    splits = lax.axis_size("tensor")
    slots_dev = stat_left.shape[0]
    rows_dev = stat_left.shape[1]
    order = stat_left.shape[2]
    blocks_group = grads.shape[0]
    shard_index = lax.axis_index("shard")
    tensor_index = lax.axis_index("tensor")
    owner_grid = owner.reshape(groups, blocks_group)
    slot_grid = slot.reshape(groups, blocks_group)
    local_owner = lax.dynamic_index_in_dim(owner_grid, shard_index, 0, keepdims=False)
    hit_mask = owner_grid == shard_index
    slot_ids = jnp.arange(slots_dev, dtype=jnp.int32)
    group_ids = jnp.arange(groups, dtype=jnp.int32)
    slot_match = jnp.any(
        (slot_grid[None, :, :] == slot_ids[:, None, None]) & hit_mask[None, :, :], axis=2
    )
    src_of_slot = jnp.argmax(slot_match, axis=1).astype(jnp.int32)
    slot_filled = jnp.any(slot_match, axis=1)
    slot_of_src = jnp.argmax(slot_match, axis=0).astype(jnp.int32)
    src_sent = jnp.any(slot_match, axis=0)
    dest_match = local_owner[None, :] == group_ids[:, None]
    block_of_dest = jnp.argmax(dest_match, axis=1).astype(jnp.int32)
    dest_used = jnp.any(dest_match, axis=1)
    row_start = tensor_index * rows_dev
    outgoing = pick(grads, block_of_dest, dest_used)
    arrived = lax.all_to_all(outgoing, "shard", split_axis=0, concat_axis=0, tiled=True)
    half = slots_dev // 2
    first_half = pick(arrived, src_of_slot[:half], slot_filled[:half])
    second_half = pick(arrived, src_of_slot[half:], slot_filled[half:])
    grad_piece = jnp.concatenate([first_half, second_half], 0)
    grad_whole = gather_rows(first_half, second_half, splits, tensor_index)
    f32 = jnp.float32
    grad_cols = lax.dynamic_slice_in_dim(grad_whole, row_start, rows_dev, 2)
    left_new = beta_stat * stat_left + (1.0 - beta_stat) * jnp.einsum(
        "kij,klj->kil", grad_piece, grad_whole, preferred_element_type=f32
    )
    right_new = beta_stat * stat_right + (1.0 - beta_stat) * jnp.einsum(
        "kji,kjl->kil", grad_cols, grad_whole, preferred_element_type=f32
    )
    grad_rows = grad_piece.astype(f32)
    second_new = beta_stat * moment + (1.0 - beta_stat) * grad_rows * grad_rows
    adam_step = grad_rows / (jnp.sqrt(second_new) + eps_root)
    three_pass = lax.DotAlgorithmPreset.BF16_BF16_F32_X3
    precond = jnp.einsum(
        "kij,kjl->kil", root_left, grad_whole.astype(f32), precision=three_pass,
        preferred_element_type=f32,
    )
    precond = jnp.einsum(
        "kij,kjl->kil", precond, root_right, precision=three_pass, preferred_element_type=f32
    )
    sums = jnp.stack(
        [jnp.sum(adam_step * adam_step, axis=(1, 2)), jnp.sum(precond * precond, axis=(1, 2))]
    )
    step = 1
    while step < splits:
        sums = sums + lax.ppermute(sums, "tensor", [(i, i ^ step) for i in range(splits)])
        step *= 2
    adam_sum, precond_sum = sums[0], sums[1]
    entries = float(rows_dev * splits * order)
    scale_ratio = jnp.sqrt(adam_sum / entries + eps_mean) / jnp.sqrt(
        precond_sum / entries + eps_mean
    )
    velocity_new = beta_mom * momentum + (1.0 - beta_mom) * scale_ratio[:, None, None] * precond
    weight_new = master - learn_rate * velocity_new
    weight_half = weight_new.astype(jnp.bfloat16)
    returning = pick(weight_half, slot_of_src, src_sent)
    back_rows = lax.all_to_all(returning, "shard", split_axis=0, concat_axis=0, tiled=True)
    weights_local = jnp.take(back_rows, local_owner, axis=0)
    return (left_new, right_new, second_new, velocity_new, weight_new, weights_local)


def solution(mesh):
    placed = (
        P("shard", "tensor", None),
        P(),
        P(),
        P("shard", "tensor", None),
        P("shard", "tensor", None),
        P("shard", "tensor", None),
        P("shard", None, None),
        P("shard", "tensor", None),
        P("shard", "tensor", None),
        P("shard", "tensor", None),
    )
    return jax.shard_map(
        on_device,
        mesh=mesh,
        in_specs=placed,
        out_specs=(
            P("shard", "tensor", None),
            P("shard", "tensor", None),
            P("shard", "tensor", None),
            P("shard", "tensor", None),
            P("shard", "tensor", None),
            P("shard", "tensor", None),
        ),
        check_vma=False,
    )
```

```python
import jax
import jax.numpy as jnp
from jax import lax
from jax.sharding import PartitionSpec as P


beta_stat = 0.95
beta_mom = 0.9
learn_rate = 0.01
eps_root = 1e-08
eps_mean = 1e-06


def gather_rows(first_half, second_half, splits):
    right = [(i, (i + 1) % splits) for i in range(splits)]
    left = [(i, (i - 1) % splits) for i in range(splits)]
    left_a = lax.ppermute(first_half, "tensor", right)
    right_b = lax.ppermute(second_half, "tensor", left)
    left_b = lax.ppermute(second_half, "tensor", right)
    right_a = lax.ppermute(first_half, "tensor", left)
    far_a = lax.ppermute(left_a, "tensor", right)
    far_b = lax.ppermute(right_b, "tensor", left)
    return (
        (first_half, second_half),
        (right_a, right_b),
        (far_a, far_b),
        (left_a, left_b),
    )


def assemble(halves_by_shift, splits, tensor_index):
    def ordered(first):
        def build():
            blocks = []
            for p in range(splits):
                shift = (p - first) % splits
                parts = [jnp.concatenate(by_shift[shift], 0) for by_shift in halves_by_shift]
                blocks.append(jnp.concatenate(parts, 1))
            return jnp.concatenate(blocks, 1)

        return build

    return lax.switch(tensor_index, [ordered(first) for first in range(splits)])


def pick(source, index, valid):
    taken = jnp.take(source, index, axis=0, mode="clip")
    return jnp.where(valid[:, None, None], taken, jnp.zeros((), source.dtype))


def on_device(
    grads, owner, slot, stat_left, stat_right, root_left, root_right, moment, momentum, master
):
    groups = lax.axis_size("shard")
    splits = lax.axis_size("tensor")
    slots_dev = stat_left.shape[0]
    rows_dev = stat_left.shape[1]
    order = stat_left.shape[2]
    blocks_group = grads.shape[0]
    shard_index = lax.axis_index("shard")
    tensor_index = lax.axis_index("tensor")
    owner_grid = owner.reshape(groups, blocks_group)
    slot_grid = slot.reshape(groups, blocks_group)
    local_owner = lax.dynamic_index_in_dim(owner_grid, shard_index, 0, keepdims=False)
    hit_mask = owner_grid == shard_index
    slot_ids = jnp.arange(slots_dev, dtype=jnp.int32)
    group_ids = jnp.arange(groups, dtype=jnp.int32)
    slot_match = jnp.any(
        (slot_grid[None, :, :] == slot_ids[:, None, None]) & hit_mask[None, :, :], axis=2
    )
    src_of_slot = jnp.argmax(slot_match, axis=1).astype(jnp.int32)
    slot_filled = jnp.any(slot_match, axis=1)
    slot_of_src = jnp.argmax(slot_match, axis=0).astype(jnp.int32)
    src_sent = jnp.any(slot_match, axis=0)
    dest_match = local_owner[None, :] == group_ids[:, None]
    block_of_dest = jnp.argmax(dest_match, axis=1).astype(jnp.int32)
    dest_used = jnp.any(dest_match, axis=1)
    row_start = tensor_index * rows_dev
    half = slots_dev // 2
    row_half = rows_dev // 2
    halves_by_shift = []
    for lo in (0, row_half):
        outgoing = pick(grads[:, lo : lo + row_half], block_of_dest, dest_used)
        arrived = lax.all_to_all(
            outgoing, "shard", split_axis=0, concat_axis=0, tiled=True
        )
        arrived, sources, filled = lax.optimization_barrier((arrived, src_of_slot, slot_filled))
        first_half = pick(arrived, sources[:half], filled[:half])
        second_half = pick(arrived, sources[half:], filled[half:])
        halves_by_shift.append(gather_rows(first_half, second_half, splits))
    grad_piece = jnp.concatenate([jnp.concatenate(h[0], 0) for h in halves_by_shift], 1)
    grad_whole = assemble(halves_by_shift, splits, tensor_index)
    f32 = jnp.float32
    grad_cols = lax.dynamic_slice_in_dim(grad_whole, row_start, rows_dev, 2)
    left_new = beta_stat * stat_left + (1.0 - beta_stat) * jnp.einsum(
        "kij,klj->kil", grad_piece, grad_whole, preferred_element_type=f32
    )
    right_new = beta_stat * stat_right + (1.0 - beta_stat) * jnp.einsum(
        "kji,kjl->kil", grad_cols, grad_whole, preferred_element_type=f32
    )
    grad_rows = grad_piece.astype(f32)
    second_new = beta_stat * moment + (1.0 - beta_stat) * grad_rows * grad_rows
    adam_step = grad_rows / (jnp.sqrt(second_new) + eps_root)
    three_pass = lax.DotAlgorithmPreset.BF16_BF16_F32_X3
    precond = jnp.einsum(
        "kij,kjl->kil", root_left, grad_whole.astype(f32), precision=three_pass,
        preferred_element_type=f32,
    )
    precond = jnp.einsum(
        "kij,kjl->kil", precond, root_right, precision=three_pass, preferred_element_type=f32
    )
    sums = jnp.stack(
        [jnp.sum(adam_step * adam_step, axis=(1, 2)), jnp.sum(precond * precond, axis=(1, 2))]
    )
    step = 1
    while step < splits:
        sums = sums + lax.ppermute(sums, "tensor", [(i, i ^ step) for i in range(splits)])
        step *= 2
    adam_sum, precond_sum = sums[0], sums[1]
    entries = float(rows_dev * splits * order)
    scale_ratio = jnp.sqrt(adam_sum / entries + eps_mean) / jnp.sqrt(
        precond_sum / entries + eps_mean
    )
    velocity_new = beta_mom * momentum + (1.0 - beta_mom) * scale_ratio[:, None, None] * precond
    weight_new = master - learn_rate * velocity_new
    weight_half = weight_new.astype(jnp.bfloat16)
    returning = pick(weight_half, slot_of_src, src_sent)
    back_rows = lax.all_to_all(returning, "shard", split_axis=0, concat_axis=0, tiled=True)
    weights_local = jnp.take(back_rows, local_owner, axis=0)
    return (left_new, right_new, second_new, velocity_new, weight_new, weights_local)


def solution(mesh):
    placed = (
        P("shard", "tensor", None),
        P(),
        P(),
        P("shard", "tensor", None),
        P("shard", "tensor", None),
        P("shard", "tensor", None),
        P("shard", None, None),
        P("shard", "tensor", None),
        P("shard", "tensor", None),
        P("shard", "tensor", None),
    )

    return jax.shard_map(
        on_device,
        mesh=mesh,
        in_specs=placed,
        out_specs=(
            P("shard", "tensor", None),
            P("shard", "tensor", None),
            P("shard", "tensor", None),
            P("shard", "tensor", None),
            P("shard", "tensor", None),
            P("shard", "tensor", None),
        ),
        check_vma=False,
    )
```

```python
import jax
import jax.numpy as jnp
from jax import lax
from jax.sharding import PartitionSpec as P


beta_stat = 0.95
beta_mom = 0.9
learn_rate = 0.01
eps_root = 1e-08
eps_mean = 1e-06


def gather_rows(first_half, second_half, splits, tensor_index):
    right = [(i, (i + 1) % splits) for i in range(splits)]
    left = [(i, (i - 1) % splits) for i in range(splits)]
    left_a = lax.ppermute(first_half, "tensor", right)
    right_b = lax.ppermute(second_half, "tensor", left)
    left_b = lax.ppermute(second_half, "tensor", right)
    right_a = lax.ppermute(first_half, "tensor", left)
    far_a = lax.ppermute(left_a, "tensor", right)
    far_b = lax.ppermute(right_b, "tensor", left)
    by_shift = (
        (first_half, second_half),
        (right_a, right_b),
        (far_a, far_b),
        (left_a, left_b),
    )

    def ordered(first):
        def build():
            rows = [jnp.concatenate(by_shift[(p - first) % splits], 0) for p in range(splits)]
            return jnp.concatenate(rows, 1)

        return build

    return lax.switch(tensor_index, [ordered(first) for first in range(splits)])


def pick(source, index, valid):
    taken = jnp.take(source, index, axis=0, mode="clip")
    return jnp.where(valid[:, None, None], taken, jnp.zeros((), source.dtype))


def on_device(
    grads, owner, slot, stat_left, stat_right, root_left, root_right, moment, momentum, master
):
    groups = lax.axis_size("shard")
    splits = lax.axis_size("tensor")
    slots_dev = stat_left.shape[0]
    rows_dev = stat_left.shape[1]
    order = stat_left.shape[2]
    blocks_group = grads.shape[0]
    shard_index = lax.axis_index("shard")
    tensor_index = lax.axis_index("tensor")
    owner_grid = owner.reshape(groups, blocks_group)
    slot_grid = slot.reshape(groups, blocks_group)
    local_owner = lax.dynamic_index_in_dim(owner_grid, shard_index, 0, keepdims=False)
    hit_mask = owner_grid == shard_index
    slot_ids = jnp.arange(slots_dev, dtype=jnp.int32)
    group_ids = jnp.arange(groups, dtype=jnp.int32)
    slot_match = jnp.any(
        (slot_grid[None, :, :] == slot_ids[:, None, None]) & hit_mask[None, :, :], axis=2
    )
    src_of_slot = jnp.argmax(slot_match, axis=1).astype(jnp.int32)
    slot_filled = jnp.any(slot_match, axis=1)
    slot_of_src = jnp.argmax(slot_match, axis=0).astype(jnp.int32)
    dest_match = local_owner[None, :] == group_ids[:, None]
    block_of_dest = jnp.argmax(dest_match, axis=1).astype(jnp.int32)
    row_start = tensor_index * rows_dev
    outgoing = jnp.take(grads, block_of_dest, axis=0, mode="clip")
    arrived = lax.all_to_all(outgoing, "shard", split_axis=0, concat_axis=0, tiled=True)
    half = slots_dev // 2
    first_half = pick(arrived, src_of_slot[:half], slot_filled[:half])
    second_half = pick(arrived, src_of_slot[half:], slot_filled[half:])
    grad_piece = jnp.concatenate([first_half, second_half], 0)
    grad_whole = gather_rows(first_half, second_half, splits, tensor_index)
    f32 = jnp.float32
    grad_cols = lax.dynamic_slice_in_dim(grad_whole, row_start, rows_dev, 2)
    left_new = beta_stat * stat_left + (1.0 - beta_stat) * jnp.einsum(
        "kij,klj->kil", grad_piece, grad_whole, preferred_element_type=f32
    )
    right_new = beta_stat * stat_right + (1.0 - beta_stat) * jnp.einsum(
        "kji,kjl->kil", grad_cols, grad_whole, preferred_element_type=f32
    )
    grad_rows = grad_piece.astype(f32)
    second_new = beta_stat * moment + (1.0 - beta_stat) * grad_rows * grad_rows
    adam_step = grad_rows / (jnp.sqrt(second_new) + eps_root)
    three_pass = lax.DotAlgorithmPreset.BF16_BF16_F32_X3
    precond = jnp.einsum(
        "kij,kjl->kil", root_left, grad_whole.astype(f32), precision=three_pass,
        preferred_element_type=f32,
    )
    precond = jnp.einsum(
        "kij,kjl->kil", precond, root_right, precision=three_pass, preferred_element_type=f32
    )
    sums = jnp.stack(
        [jnp.sum(adam_step * adam_step, axis=(1, 2)), jnp.sum(precond * precond, axis=(1, 2))]
    )
    step = 1
    while step < splits:
        sums = sums + lax.ppermute(sums, "tensor", [(i, i ^ step) for i in range(splits)])
        step *= 2
    adam_sum, precond_sum = sums[0], sums[1]
    entries = float(rows_dev * splits * order)
    scale_ratio = jnp.sqrt(adam_sum / entries + eps_mean) / jnp.sqrt(
        precond_sum / entries + eps_mean
    )
    velocity_new = beta_mom * momentum + (1.0 - beta_mom) * scale_ratio[:, None, None] * precond
    weight_new = master - learn_rate * velocity_new
    weight_half = weight_new.astype(jnp.bfloat16)
    returning = jnp.take(weight_half, slot_of_src, axis=0, mode="clip")
    back_rows = lax.all_to_all(returning, "shard", split_axis=0, concat_axis=0, tiled=True)
    weights_local = jnp.take(back_rows, local_owner, axis=0, mode="clip")
    return (left_new, right_new, second_new, velocity_new, weight_new, weights_local)


def solution(mesh):
    placed = (
        P("shard", "tensor", None),
        P(),
        P(),
        P("shard", "tensor", None),
        P("shard", "tensor", None),
        P("shard", "tensor", None),
        P("shard", None, None),
        P("shard", "tensor", None),
        P("shard", "tensor", None),
        P("shard", "tensor", None),
    )

    return jax.shard_map(
        on_device,
        mesh=mesh,
        in_specs=placed,
        out_specs=(
            P("shard", "tensor", None),
            P("shard", "tensor", None),
            P("shard", "tensor", None),
            P("shard", "tensor", None),
            P("shard", "tensor", None),
            P("shard", "tensor", None),
        ),
        check_vma=False,
    )
```

```python
import jax
import jax.numpy as jnp
from jax import lax
from jax.sharding import PartitionSpec as P


beta_stat = 0.95
beta_mom = 0.9
learn_rate = 0.01
eps_root = 1e-08
eps_mean = 1e-06


def gather_rows(piece, far_right, splits, tensor_index):
    right = [(i, (i + 1) % splits) for i in range(splits)]
    left = [(i, (i - 1) % splits) for i in range(splits)]
    from_left = lax.ppermute(piece, "tensor", right)
    from_right = lax.ppermute(piece, "tensor", left)
    if far_right:
        far = lax.ppermute(from_left, "tensor", right)
    else:
        far = lax.ppermute(from_right, "tensor", left)
    by_shift = (piece, from_right, far, from_left)

    def ordered(first):
        return lambda: jnp.concatenate([by_shift[(p - first) % splits] for p in range(splits)], 1)

    return lax.switch(tensor_index, [ordered(first) for first in range(splits)])


def pick(source, index, valid):
    taken = jnp.take(source, index, axis=0, mode="clip")
    return jnp.where(valid[:, None, None], taken, jnp.zeros((), source.dtype))


def on_device(
    grads, owner, slot, stat_left, stat_right, root_left, root_right, moment, momentum, master
):
    groups = lax.axis_size("shard")
    splits = lax.axis_size("tensor")
    slots_dev = stat_left.shape[0]
    rows_dev = stat_left.shape[1]
    order = stat_left.shape[2]
    blocks_group = grads.shape[0]
    shard_index = lax.axis_index("shard")
    tensor_index = lax.axis_index("tensor")
    owner_grid = owner.reshape(groups, blocks_group)
    slot_grid = slot.reshape(groups, blocks_group)
    local_owner = lax.dynamic_index_in_dim(owner_grid, shard_index, 0, keepdims=False)
    hit_mask = owner_grid == shard_index
    slot_ids = jnp.arange(slots_dev, dtype=jnp.int32)
    group_ids = jnp.arange(groups, dtype=jnp.int32)
    slot_match = jnp.any(
        (slot_grid[None, :, :] == slot_ids[:, None, None]) & hit_mask[None, :, :], axis=2
    )
    src_of_slot = jnp.argmax(slot_match, axis=1).astype(jnp.int32)
    slot_filled = jnp.any(slot_match, axis=1)
    slot_of_src = jnp.argmax(slot_match, axis=0).astype(jnp.int32)
    src_sent = jnp.any(slot_match, axis=0)
    dest_match = local_owner[None, :] == group_ids[:, None]
    block_of_dest = jnp.argmax(dest_match, axis=1).astype(jnp.int32)
    dest_used = jnp.any(dest_match, axis=1)
    row_start = tensor_index * rows_dev
    outgoing = pick(grads, block_of_dest, dest_used)
    arrived = lax.all_to_all(outgoing, "shard", split_axis=0, concat_axis=0, tiled=True)
    half = slots_dev // 2
    first_half = pick(arrived, src_of_slot[:half], slot_filled[:half])
    second_half = pick(arrived, src_of_slot[half:], slot_filled[half:])
    grad_piece = jnp.concatenate([first_half, second_half], 0)
    whole_halves = [
        gather_rows(first_half, True, splits, tensor_index),
        gather_rows(second_half, False, splits, tensor_index),
    ]
    grad_whole = jnp.concatenate(whole_halves, 0)
    f32 = jnp.float32
    grad_cols = lax.dynamic_slice_in_dim(grad_whole, row_start, rows_dev, 2)
    left_new = beta_stat * stat_left + (1.0 - beta_stat) * jnp.einsum(
        "kij,klj->kil", grad_piece, grad_whole, preferred_element_type=f32
    )
    right_new = beta_stat * stat_right + (1.0 - beta_stat) * jnp.einsum(
        "kji,kjl->kil", grad_cols, grad_whole, preferred_element_type=f32
    )
    grad_rows = grad_piece.astype(f32)
    second_new = beta_stat * moment + (1.0 - beta_stat) * grad_rows * grad_rows
    adam_step = grad_rows / (jnp.sqrt(second_new) + eps_root)
    three_pass = lax.DotAlgorithmPreset.BF16_BF16_F32_X3
    precond_parts = []
    for part, whole in enumerate(whole_halves):
        lo = part * half
        mixed = jnp.einsum(
            "kij,kjl->kil", root_left[lo : lo + half], whole.astype(f32),
            precision=three_pass, preferred_element_type=f32,
        )
        precond_parts.append(jnp.einsum(
            "kij,kjl->kil", mixed, root_right[lo : lo + half], precision=three_pass,
            preferred_element_type=f32,
        ))
    precond = jnp.concatenate(precond_parts, 0)
    precond_sq = jnp.concatenate([jnp.sum(p * p, axis=(1, 2)) for p in precond_parts])
    sums = jnp.stack(
        [jnp.sum(adam_step * adam_step, axis=(1, 2)), precond_sq]
    )
    step = 1
    while step < splits:
        sums = sums + lax.ppermute(sums, "tensor", [(i, i ^ step) for i in range(splits)])
        step *= 2
    adam_sum, precond_sum = sums[0], sums[1]
    entries = float(rows_dev * splits * order)
    scale_ratio = jnp.sqrt(adam_sum / entries + eps_mean) / jnp.sqrt(
        precond_sum / entries + eps_mean
    )
    velocity_new = beta_mom * momentum + (1.0 - beta_mom) * scale_ratio[:, None, None] * precond
    weight_new = master - learn_rate * velocity_new
    weight_half = weight_new.astype(jnp.bfloat16)
    returning = pick(weight_half, slot_of_src, src_sent)
    back_rows = lax.all_to_all(returning, "shard", split_axis=0, concat_axis=0, tiled=True)
    weights_local = jnp.take(back_rows, local_owner, axis=0)
    return (left_new, right_new, second_new, velocity_new, weight_new, weights_local)


def solution(mesh):
    placed = (
        P("shard", "tensor", None),
        P(),
        P(),
        P("shard", "tensor", None),
        P("shard", "tensor", None),
        P("shard", "tensor", None),
        P("shard", None, None),
        P("shard", "tensor", None),
        P("shard", "tensor", None),
        P("shard", "tensor", None),
    )

    return jax.shard_map(
        on_device,
        mesh=mesh,
        in_specs=placed,
        out_specs=(
            P("shard", "tensor", None),
            P("shard", "tensor", None),
            P("shard", "tensor", None),
            P("shard", "tensor", None),
            P("shard", "tensor", None),
            P("shard", "tensor", None),
        ),
        check_vma=False,
    )
```

```python
import jax
import jax.numpy as jnp
from jax import lax
from jax.sharding import PartitionSpec as P


beta_stat = 0.95
beta_mom = 0.9
learn_rate = 0.01
eps_root = 1e-08
eps_mean = 1e-06


def gather_rows(piece, far_right, splits, tensor_index):
    right = [(i, (i + 1) % splits) for i in range(splits)]
    left = [(i, (i - 1) % splits) for i in range(splits)]
    from_left = lax.ppermute(piece, "tensor", right)
    from_right = lax.ppermute(piece, "tensor", left)
    if far_right:
        far = lax.ppermute(from_left, "tensor", right)
    else:
        far = lax.ppermute(from_right, "tensor", left)
    by_shift = (piece, from_right, far, from_left)

    def ordered(first):
        return lambda: jnp.concatenate([by_shift[(p - first) % splits] for p in range(splits)], 1)

    return lax.switch(tensor_index, [ordered(first) for first in range(splits)])


def pick(source, index, valid):
    taken = source.at[index].get(mode="promise_in_bounds")
    return jnp.where(valid[:, None, None], taken, jnp.zeros((), source.dtype))


def on_device(
    grads, owner, slot, stat_left, stat_right, root_left, root_right, moment, momentum, master
):
    groups = lax.axis_size("shard")
    splits = lax.axis_size("tensor")
    slots_dev = stat_left.shape[0]
    rows_dev = stat_left.shape[1]
    order = stat_left.shape[2]
    blocks_group = grads.shape[0]
    shard_index = lax.axis_index("shard")
    tensor_index = lax.axis_index("tensor")
    owner_grid = owner.reshape(groups, blocks_group)
    slot_grid = slot.reshape(groups, blocks_group)
    local_owner = lax.dynamic_index_in_dim(owner_grid, shard_index, 0, keepdims=False)
    hit_mask = owner_grid == shard_index
    slot_ids = jnp.arange(slots_dev, dtype=jnp.int32)
    group_ids = jnp.arange(groups, dtype=jnp.int32)
    slot_match = jnp.any(
        (slot_grid[None, :, :] == slot_ids[:, None, None]) & hit_mask[None, :, :], axis=2
    )
    src_of_slot = jnp.argmax(slot_match, axis=1).astype(jnp.int32)
    slot_filled = jnp.any(slot_match, axis=1)
    slot_of_src = jnp.argmax(slot_match, axis=0).astype(jnp.int32)
    dest_match = local_owner[None, :] == group_ids[:, None]
    block_of_dest = jnp.argmax(dest_match, axis=1).astype(jnp.int32)
    dest_used = jnp.any(dest_match, axis=1)
    row_start = tensor_index * rows_dev
    outgoing = pick(grads, block_of_dest, dest_used)
    arrived = lax.all_to_all(outgoing, "shard", split_axis=0, concat_axis=0, tiled=True)
    half = slots_dev // 2
    first_half = pick(arrived, src_of_slot[:half], slot_filled[:half])
    second_half = pick(arrived, src_of_slot[half:], slot_filled[half:])
    grad_piece = jnp.concatenate([first_half, second_half], 0)
    whole_halves = [
        gather_rows(first_half, True, splits, tensor_index),
        gather_rows(second_half, False, splits, tensor_index),
    ]
    grad_whole = jnp.concatenate(whole_halves, 0)
    f32 = jnp.float32
    grad_cols = lax.dynamic_slice_in_dim(grad_whole, row_start, rows_dev, 2)
    left_new = beta_stat * stat_left + (1.0 - beta_stat) * jnp.einsum(
        "kij,klj->kil", grad_piece, grad_whole, preferred_element_type=f32
    )
    right_new = beta_stat * stat_right + (1.0 - beta_stat) * jnp.einsum(
        "kji,kjl->kil", grad_cols, grad_whole, preferred_element_type=f32
    )
    grad_rows = grad_piece.astype(f32)
    second_new = beta_stat * moment + (1.0 - beta_stat) * grad_rows * grad_rows
    adam_step = grad_rows / (jnp.sqrt(second_new) + eps_root)
    three_pass = lax.DotAlgorithmPreset.BF16_BF16_F32_X3
    precond_parts = []
    for part, whole in enumerate(whole_halves):
        lo = part * half
        mixed = jnp.einsum(
            "kij,kjl->kil", root_left[lo : lo + half], whole.astype(f32),
            precision=three_pass, preferred_element_type=f32,
        )
        precond_parts.append(jnp.einsum(
            "kij,kjl->kil", mixed, root_right[lo : lo + half], precision=three_pass,
            preferred_element_type=f32,
        ))
    precond = jnp.concatenate(precond_parts, 0)
    precond_sq = jnp.concatenate([jnp.sum(p * p, axis=(1, 2)) for p in precond_parts])
    sums = jnp.stack(
        [jnp.sum(adam_step * adam_step, axis=(1, 2)), precond_sq]
    )
    step = 1
    while step < splits:
        sums = sums + lax.ppermute(sums, "tensor", [(i, i ^ step) for i in range(splits)])
        step *= 2
    adam_sum, precond_sum = sums[0], sums[1]
    entries = float(rows_dev * splits * order)
    scale_ratio = jnp.sqrt(adam_sum / entries + eps_mean) / jnp.sqrt(
        precond_sum / entries + eps_mean
    )
    velocity_new = beta_mom * momentum + (1.0 - beta_mom) * scale_ratio[:, None, None] * precond
    weight_new = master - learn_rate * velocity_new
    weight_half = weight_new.astype(jnp.bfloat16)
    returning = weight_half.at[slot_of_src].get(mode="promise_in_bounds")
    back_rows = lax.all_to_all(returning, "shard", split_axis=0, concat_axis=0, tiled=True)
    weights_local = back_rows.at[local_owner].get(mode="promise_in_bounds")
    return (left_new, right_new, second_new, velocity_new, weight_new, weights_local)


def solution(mesh):
    placed = (
        P("shard", "tensor", None),
        P(),
        P(),
        P("shard", "tensor", None),
        P("shard", "tensor", None),
        P("shard", "tensor", None),
        P("shard", None, None),
        P("shard", "tensor", None),
        P("shard", "tensor", None),
        P("shard", "tensor", None),
    )

    return jax.shard_map(
        on_device,
        mesh=mesh,
        in_specs=placed,
        out_specs=(
            P("shard", "tensor", None),
            P("shard", "tensor", None),
            P("shard", "tensor", None),
            P("shard", "tensor", None),
            P("shard", "tensor", None),
            P("shard", "tensor", None),
        ),
        check_vma=False,
    )
```

```python
import jax
import jax.numpy as jnp
from jax import lax
from jax.sharding import PartitionSpec as P


beta_stat = 0.95
beta_mom = 0.9
learn_rate = 0.01
eps_root = 1e-08
eps_mean = 1e-06


def gather_rows(piece, splits, tensor_index):
    right = [(i, (i + 1) % splits) for i in range(splits)]
    left = [(i, (i - 1) % splits) for i in range(splits)]
    from_left = lax.ppermute(piece, "tensor", right)
    from_right = lax.ppermute(piece, "tensor", left)
    cut = piece.shape[0] // 2
    far = jnp.concatenate(
        [
            lax.ppermute(from_left[:cut], "tensor", right),
            lax.ppermute(from_right[cut:], "tensor", left),
        ],
        0,
    )
    by_shift = (piece, from_right, far, from_left)

    def ordered(first):
        return lambda: jnp.concatenate([by_shift[(p - first) % splits] for p in range(splits)], 1)

    return lax.switch(tensor_index, [ordered(first) for first in range(splits)])


def pick(source, index, valid):
    taken = jnp.take(source, index, axis=0, mode="clip")
    return jnp.where(valid[:, None, None], taken, jnp.zeros((), source.dtype))


def on_device(
    grads, owner, slot, stat_left, stat_right, root_left, root_right, moment, momentum, master
):
    groups = lax.axis_size("shard")
    splits = lax.axis_size("tensor")
    slots_dev = stat_left.shape[0]
    rows_dev = stat_left.shape[1]
    order = stat_left.shape[2]
    blocks_group = grads.shape[0]
    shard_index = lax.axis_index("shard")
    tensor_index = lax.axis_index("tensor")
    owner_grid = owner.reshape(groups, blocks_group)
    slot_grid = slot.reshape(groups, blocks_group)
    local_owner = lax.dynamic_index_in_dim(owner_grid, shard_index, 0, keepdims=False)
    hit_mask = owner_grid == shard_index
    slot_ids = jnp.arange(slots_dev, dtype=jnp.int32)
    group_ids = jnp.arange(groups, dtype=jnp.int32)
    slot_match = jnp.any(
        (slot_grid[None, :, :] == slot_ids[:, None, None]) & hit_mask[None, :, :], axis=2
    )
    src_of_slot = jnp.argmax(slot_match, axis=1).astype(jnp.int32)
    slot_filled = jnp.any(slot_match, axis=1)
    slot_of_src = jnp.argmax(slot_match, axis=0).astype(jnp.int32)
    dest_match = local_owner[None, :] == group_ids[:, None]
    block_of_dest = jnp.argmax(dest_match, axis=1).astype(jnp.int32)
    dest_used = jnp.any(dest_match, axis=1)
    row_start = tensor_index * rows_dev
    outgoing = pick(grads, block_of_dest, dest_used)
    arrived = lax.all_to_all(outgoing, "shard", split_axis=0, concat_axis=0, tiled=True)
    half = (2 * slots_dev) // 3
    first_half = pick(arrived, src_of_slot[:half], slot_filled[:half])
    second_half = pick(arrived, src_of_slot[half:], slot_filled[half:])
    grad_piece = jnp.concatenate([first_half, second_half], 0)
    whole_halves = [
        gather_rows(first_half, splits, tensor_index),
        gather_rows(second_half, splits, tensor_index),
    ]
    grad_whole = jnp.concatenate(whole_halves, 0)
    f32 = jnp.float32
    grad_cols = lax.dynamic_slice_in_dim(grad_whole, row_start, rows_dev, 2)
    left_new = beta_stat * stat_left + (1.0 - beta_stat) * jnp.einsum(
        "kij,klj->kil", grad_piece, grad_whole, preferred_element_type=f32
    )
    right_new = beta_stat * stat_right + (1.0 - beta_stat) * jnp.einsum(
        "kji,kjl->kil", grad_cols, grad_whole, preferred_element_type=f32
    )
    grad_rows = grad_piece.astype(f32)
    second_new = beta_stat * moment + (1.0 - beta_stat) * grad_rows * grad_rows
    adam_step = grad_rows / (jnp.sqrt(second_new) + eps_root)
    three_pass = lax.DotAlgorithmPreset.BF16_BF16_F32_X3
    precond_parts = []
    for part, whole in enumerate(whole_halves):
        lo = part * half
        hi = lo + whole.shape[0]
        mixed = jnp.einsum(
            "kij,kjl->kil", root_left[lo:hi], whole.astype(f32),
            precision=three_pass, preferred_element_type=f32,
        )
        precond_parts.append(jnp.einsum(
            "kij,kjl->kil", mixed, root_right[lo:hi], precision=three_pass,
            preferred_element_type=f32,
        ))
    precond = jnp.concatenate(precond_parts, 0)
    precond_sq = jnp.concatenate([jnp.sum(p * p, axis=(1, 2)) for p in precond_parts])
    sums = jnp.stack(
        [jnp.sum(adam_step * adam_step, axis=(1, 2)), precond_sq]
    )
    step = 1
    while step < splits:
        sums = sums + lax.ppermute(sums, "tensor", [(i, i ^ step) for i in range(splits)])
        step *= 2
    adam_sum, precond_sum = sums[0], sums[1]
    entries = float(rows_dev * splits * order)
    scale_ratio = jnp.sqrt(adam_sum / entries + eps_mean) / jnp.sqrt(
        precond_sum / entries + eps_mean
    )
    velocity_new = beta_mom * momentum + (1.0 - beta_mom) * scale_ratio[:, None, None] * precond
    weight_new = master - learn_rate * velocity_new
    weight_half = weight_new.astype(jnp.bfloat16)
    returning = jnp.take(weight_half, slot_of_src, axis=0, mode="clip")
    back_rows = lax.all_to_all(returning, "shard", split_axis=0, concat_axis=0, tiled=True)
    weights_local = jnp.take(back_rows, local_owner, axis=0, mode="clip")
    return (left_new, right_new, second_new, velocity_new, weight_new, weights_local)


def solution(mesh):
    placed = (
        P("shard", "tensor", None),
        P(),
        P(),
        P("shard", "tensor", None),
        P("shard", "tensor", None),
        P("shard", "tensor", None),
        P("shard", None, None),
        P("shard", "tensor", None),
        P("shard", "tensor", None),
        P("shard", "tensor", None),
    )

    return jax.shard_map(
        on_device,
        mesh=mesh,
        in_specs=placed,
        out_specs=(
            P("shard", "tensor", None),
            P("shard", "tensor", None),
            P("shard", "tensor", None),
            P("shard", "tensor", None),
            P("shard", "tensor", None),
            P("shard", "tensor", None),
        ),
        check_vma=False,
    )
```

```python
import jax
import jax.numpy as jnp
from jax import lax
from jax.sharding import PartitionSpec as P


beta_stat = 0.95
beta_mom = 0.9
learn_rate = 0.01
eps_root = 1e-08
eps_mean = 1e-06


def gather_rows(piece, far_right, splits, tensor_index):
    right = [(i, (i + 1) % splits) for i in range(splits)]
    left = [(i, (i - 1) % splits) for i in range(splits)]
    from_left = lax.ppermute(piece, "tensor", right)
    from_right = lax.ppermute(piece, "tensor", left)
    if far_right:
        far = lax.ppermute(from_left, "tensor", right)
    else:
        far = lax.ppermute(from_right, "tensor", left)
    by_shift = (piece, from_right, far, from_left)

    def ordered(first):
        return lambda: jnp.concatenate([by_shift[(p - first) % splits] for p in range(splits)], 1)

    return lax.switch(tensor_index, [ordered(first) for first in range(splits)])


def pick(source, index, valid):
    taken = jnp.take(source, index, axis=0, mode="clip")
    return jnp.where(valid[:, None, None], taken, jnp.zeros((), source.dtype))


def on_device(
    grads, owner, slot, stat_left, stat_right, root_left, root_right, moment, momentum, master
):
    groups = lax.axis_size("shard")
    splits = lax.axis_size("tensor")
    slots_dev = stat_left.shape[0]
    rows_dev = stat_left.shape[1]
    order = stat_left.shape[2]
    blocks_group = grads.shape[0]
    shard_index = lax.axis_index("shard")
    tensor_index = lax.axis_index("tensor")
    owner_grid = owner.reshape(groups, blocks_group)
    slot_grid = slot.reshape(groups, blocks_group)
    local_owner = lax.dynamic_index_in_dim(owner_grid, shard_index, 0, keepdims=False)
    hit_mask = owner_grid == shard_index
    slot_ids = jnp.arange(slots_dev, dtype=jnp.int32)
    group_ids = jnp.arange(groups, dtype=jnp.int32)
    slot_match = jnp.any(
        (slot_grid[None, :, :] == slot_ids[:, None, None]) & hit_mask[None, :, :], axis=2
    )
    src_of_slot = jnp.argmax(slot_match, axis=1).astype(jnp.int32)
    slot_filled = jnp.any(slot_match, axis=1)
    slot_of_src = jnp.argmax(slot_match, axis=0).astype(jnp.int32)
    dest_match = local_owner[None, :] == group_ids[:, None]
    block_of_dest = jnp.argmax(dest_match, axis=1).astype(jnp.int32)
    dest_used = jnp.any(dest_match, axis=1)
    row_start = tensor_index * rows_dev
    outgoing = pick(grads, block_of_dest, dest_used)
    arrived = lax.all_to_all(outgoing, "shard", split_axis=0, concat_axis=0, tiled=True)
    half = slots_dev // 2
    first_half = pick(arrived, src_of_slot[:half], slot_filled[:half])
    second_half = pick(arrived, src_of_slot[half:], slot_filled[half:])
    grad_piece = jnp.concatenate([first_half, second_half], 0)
    whole_halves = [
        gather_rows(first_half, True, splits, tensor_index),
        gather_rows(second_half, False, splits, tensor_index),
    ]
    grad_whole = jnp.concatenate(whole_halves, 0)
    f32 = jnp.float32
    grad_cols = lax.dynamic_slice_in_dim(grad_whole, row_start, rows_dev, 2)
    left_new = beta_stat * stat_left + (1.0 - beta_stat) * jnp.einsum(
        "kij,klj->kil", grad_piece, grad_whole, preferred_element_type=f32
    )
    right_new = beta_stat * stat_right + (1.0 - beta_stat) * jnp.einsum(
        "kji,kjl->kil", grad_cols, grad_whole, preferred_element_type=f32
    )
    grad_rows = grad_piece.astype(f32)
    second_new = beta_stat * moment + (1.0 - beta_stat) * grad_rows * grad_rows
    adam_step = grad_rows / (jnp.sqrt(second_new) + eps_root)
    three_pass = lax.DotAlgorithmPreset.BF16_BF16_F32_X3
    precond_parts = []
    for part, whole in enumerate(whole_halves):
        lo = part * half
        root = root_left[lo : lo + half]
        root_hi = root.astype(jnp.bfloat16)
        rest = root - root_hi.astype(f32)
        root_mid = rest.astype(jnp.bfloat16)
        root_lo = (rest - root_mid.astype(f32)).astype(jnp.bfloat16)
        mixed = sum(
            jnp.einsum("kij,kjl->kil", part_bf, whole, preferred_element_type=f32)
            for part_bf in (root_hi, root_mid, root_lo)
        )
        precond_parts.append(jnp.einsum(
            "kij,kjl->kil", mixed, root_right[lo : lo + half], precision=three_pass,
            preferred_element_type=f32,
        ))
    precond = jnp.concatenate(precond_parts, 0)
    precond_sq = jnp.concatenate([jnp.sum(p * p, axis=(1, 2)) for p in precond_parts])
    sums = jnp.stack(
        [jnp.sum(adam_step * adam_step, axis=(1, 2)), precond_sq]
    )
    step = 1
    while step < splits:
        sums = sums + lax.ppermute(sums, "tensor", [(i, i ^ step) for i in range(splits)])
        step *= 2
    adam_sum, precond_sum = sums[0], sums[1]
    entries = float(rows_dev * splits * order)
    scale_ratio = jnp.sqrt(adam_sum / entries + eps_mean) / jnp.sqrt(
        precond_sum / entries + eps_mean
    )
    velocity_new = beta_mom * momentum + (1.0 - beta_mom) * scale_ratio[:, None, None] * precond
    weight_new = master - learn_rate * velocity_new
    weight_half = weight_new.astype(jnp.bfloat16)
    returning = jnp.take(weight_half, slot_of_src, axis=0, mode="clip")
    back_rows = lax.all_to_all(returning, "shard", split_axis=0, concat_axis=0, tiled=True)
    weights_local = jnp.take(back_rows, local_owner, axis=0, mode="clip")
    return (left_new, right_new, second_new, velocity_new, weight_new, weights_local)


def solution(mesh):
    placed = (
        P("shard", "tensor", None),
        P(),
        P(),
        P("shard", "tensor", None),
        P("shard", "tensor", None),
        P("shard", "tensor", None),
        P("shard", None, None),
        P("shard", "tensor", None),
        P("shard", "tensor", None),
        P("shard", "tensor", None),
    )

    return jax.shard_map(
        on_device,
        mesh=mesh,
        in_specs=placed,
        out_specs=(
            P("shard", "tensor", None),
            P("shard", "tensor", None),
            P("shard", "tensor", None),
            P("shard", "tensor", None),
            P("shard", "tensor", None),
            P("shard", "tensor", None),
        ),
        check_vma=False,
    )
```

```python
import jax
import jax.numpy as jnp
from jax import lax
from jax.sharding import PartitionSpec as P


beta_stat = 0.95
beta_mom = 0.9
learn_rate = 0.01
eps_root = 1e-08
eps_mean = 1e-06


def gather_rows(piece, far_right, splits, tensor_index):
    right = [(i, (i + 1) % splits) for i in range(splits)]
    left = [(i, (i - 1) % splits) for i in range(splits)]
    from_left = lax.ppermute(piece, "tensor", right)
    from_right = lax.ppermute(piece, "tensor", left)
    if far_right:
        far = lax.ppermute(from_left, "tensor", right)
    else:
        far = lax.ppermute(from_right, "tensor", left)
    by_shift = (piece, from_right, far, from_left)

    def ordered(first):
        return lambda: jnp.concatenate([by_shift[(p - first) % splits] for p in range(splits)], 1)

    return lax.switch(tensor_index, [ordered(first) for first in range(splits)])


def pick(source, index, valid):
    ids = jnp.arange(source.shape[0], dtype=jnp.int32)
    chooser = ((index[:, None] == ids[None, :]) & valid[:, None]).astype(source.dtype)
    flat = source.reshape(source.shape[0], -1)
    taken = jnp.dot(chooser, flat, preferred_element_type=jnp.float32).astype(source.dtype)
    return taken.reshape((index.shape[0],) + source.shape[1:])


def on_device(
    grads, owner, slot, stat_left, stat_right, root_left, root_right, moment, momentum, master
):
    groups = lax.axis_size("shard")
    splits = lax.axis_size("tensor")
    slots_dev = stat_left.shape[0]
    rows_dev = stat_left.shape[1]
    order = stat_left.shape[2]
    blocks_group = grads.shape[0]
    shard_index = lax.axis_index("shard")
    tensor_index = lax.axis_index("tensor")
    owner_grid = owner.reshape(groups, blocks_group)
    slot_grid = slot.reshape(groups, blocks_group)
    local_owner = lax.dynamic_index_in_dim(owner_grid, shard_index, 0, keepdims=False)
    hit_mask = owner_grid == shard_index
    slot_ids = jnp.arange(slots_dev, dtype=jnp.int32)
    group_ids = jnp.arange(groups, dtype=jnp.int32)
    slot_match = jnp.any(
        (slot_grid[None, :, :] == slot_ids[:, None, None]) & hit_mask[None, :, :], axis=2
    )
    src_of_slot = jnp.argmax(slot_match, axis=1).astype(jnp.int32)
    slot_filled = jnp.any(slot_match, axis=1)
    slot_of_src = jnp.argmax(slot_match, axis=0).astype(jnp.int32)
    dest_match = local_owner[None, :] == group_ids[:, None]
    block_of_dest = jnp.argmax(dest_match, axis=1).astype(jnp.int32)
    dest_used = jnp.any(dest_match, axis=1)
    row_start = tensor_index * rows_dev
    outgoing = pick(grads, block_of_dest, dest_used)
    arrived = lax.all_to_all(outgoing, "shard", split_axis=0, concat_axis=0, tiled=True)
    half = slots_dev // 2
    first_half = pick(arrived, src_of_slot[:half], slot_filled[:half])
    second_half = pick(arrived, src_of_slot[half:], slot_filled[half:])
    grad_piece = jnp.concatenate([first_half, second_half], 0)
    whole_halves = [
        gather_rows(first_half, True, splits, tensor_index),
        gather_rows(second_half, False, splits, tensor_index),
    ]
    grad_whole = jnp.concatenate(whole_halves, 0)
    f32 = jnp.float32
    grad_cols = lax.dynamic_slice_in_dim(grad_whole, row_start, rows_dev, 2)
    left_new = beta_stat * stat_left + (1.0 - beta_stat) * jnp.einsum(
        "kij,klj->kil", grad_piece, grad_whole, preferred_element_type=f32
    )
    right_new = beta_stat * stat_right + (1.0 - beta_stat) * jnp.einsum(
        "kji,kjl->kil", grad_cols, grad_whole, preferred_element_type=f32
    )
    grad_rows = grad_piece.astype(f32)
    second_new = beta_stat * moment + (1.0 - beta_stat) * grad_rows * grad_rows
    adam_step = grad_rows / (jnp.sqrt(second_new) + eps_root)
    three_pass = lax.DotAlgorithmPreset.BF16_BF16_F32_X3
    precond_parts = []
    for part, whole in enumerate(whole_halves):
        lo = part * half
        mixed = jnp.einsum(
            "kij,kjl->kil", root_left[lo : lo + half], whole.astype(f32),
            precision=three_pass, preferred_element_type=f32,
        )
        precond_parts.append(jnp.einsum(
            "kij,kjl->kil", mixed, root_right[lo : lo + half], precision=three_pass,
            preferred_element_type=f32,
        ))
    precond = jnp.concatenate(precond_parts, 0)
    precond_sq = jnp.concatenate([jnp.sum(p * p, axis=(1, 2)) for p in precond_parts])
    sums = jnp.stack(
        [jnp.sum(adam_step * adam_step, axis=(1, 2)), precond_sq]
    )
    step = 1
    while step < splits:
        sums = sums + lax.ppermute(sums, "tensor", [(i, i ^ step) for i in range(splits)])
        step *= 2
    adam_sum, precond_sum = sums[0], sums[1]
    entries = float(rows_dev * splits * order)
    scale_ratio = jnp.sqrt(adam_sum / entries + eps_mean) / jnp.sqrt(
        precond_sum / entries + eps_mean
    )
    velocity_new = beta_mom * momentum + (1.0 - beta_mom) * scale_ratio[:, None, None] * precond
    weight_new = master - learn_rate * velocity_new
    weight_half = weight_new.astype(jnp.bfloat16)
    returning = pick(weight_half, slot_of_src, jnp.any(slot_match, axis=0))
    back_rows = lax.all_to_all(returning, "shard", split_axis=0, concat_axis=0, tiled=True)
    weights_local = pick(back_rows, local_owner, jnp.ones(local_owner.shape, jnp.bool_))
    return (left_new, right_new, second_new, velocity_new, weight_new, weights_local)


def solution(mesh):
    placed = (
        P("shard", "tensor", None),
        P(),
        P(),
        P("shard", "tensor", None),
        P("shard", "tensor", None),
        P("shard", "tensor", None),
        P("shard", None, None),
        P("shard", "tensor", None),
        P("shard", "tensor", None),
        P("shard", "tensor", None),
    )

    return jax.shard_map(
        on_device,
        mesh=mesh,
        in_specs=placed,
        out_specs=(
            P("shard", "tensor", None),
            P("shard", "tensor", None),
            P("shard", "tensor", None),
            P("shard", "tensor", None),
            P("shard", "tensor", None),
            P("shard", "tensor", None),
        ),
        check_vma=False,
    )
```

```python
import jax
import jax.numpy as jnp
from jax import lax
from jax.sharding import PartitionSpec as P


beta_stat = 0.95
beta_mom = 0.9
learn_rate = 0.01
eps_root = 1e-08
eps_mean = 1e-06


def gather_rows(piece, splits, tensor_index):
    right = [(i, (i + 1) % splits) for i in range(splits)]
    left = [(i, (i - 1) % splits) for i in range(splits)]
    from_left = lax.ppermute(piece, "tensor", right)
    from_right = lax.ppermute(piece, "tensor", left)
    cut = piece.shape[0] // 2
    far = jnp.concatenate(
        [
            lax.ppermute(from_left[:cut], "tensor", right),
            lax.ppermute(from_right[cut:], "tensor", left),
        ],
        0,
    )
    by_shift = (piece, from_right, far, from_left)

    def ordered(first):
        return lambda: jnp.concatenate([by_shift[(p - first) % splits] for p in range(splits)], 1)

    return lax.switch(tensor_index, [ordered(first) for first in range(splits)])


def pick(source, index, valid):
    taken = jnp.take(source, index, axis=0, mode="clip")
    return jnp.where(valid[:, None, None], taken, jnp.zeros((), source.dtype))


def on_device(
    grads, owner, slot, stat_left, stat_right, root_left, root_right, moment, momentum, master
):
    groups = lax.axis_size("shard")
    splits = lax.axis_size("tensor")
    slots_dev = stat_left.shape[0]
    rows_dev = stat_left.shape[1]
    order = stat_left.shape[2]
    blocks_group = grads.shape[0]
    shard_index = lax.axis_index("shard")
    tensor_index = lax.axis_index("tensor")
    owner_grid = owner.reshape(groups, blocks_group)
    slot_grid = slot.reshape(groups, blocks_group)
    local_owner = lax.dynamic_index_in_dim(owner_grid, shard_index, 0, keepdims=False)
    hit_mask = owner_grid == shard_index
    slot_ids = jnp.arange(slots_dev, dtype=jnp.int32)
    group_ids = jnp.arange(groups, dtype=jnp.int32)
    slot_match = jnp.any(
        (slot_grid[None, :, :] == slot_ids[:, None, None]) & hit_mask[None, :, :], axis=2
    )
    src_of_slot = jnp.argmax(slot_match, axis=1).astype(jnp.int32)
    slot_filled = jnp.any(slot_match, axis=1)
    slot_of_src = jnp.argmax(slot_match, axis=0).astype(jnp.int32)
    dest_match = local_owner[None, :] == group_ids[:, None]
    block_of_dest = jnp.argmax(dest_match, axis=1).astype(jnp.int32)
    dest_used = jnp.any(dest_match, axis=1)
    row_start = tensor_index * rows_dev
    outgoing = pick(grads, block_of_dest, dest_used)
    arrived = lax.all_to_all(outgoing, "shard", split_axis=0, concat_axis=0, tiled=True)
    half = (2 * slots_dev) // 3
    first_half = pick(arrived, src_of_slot[:half], slot_filled[:half])
    second_half = pick(arrived, src_of_slot[half:], slot_filled[half:])
    grad_piece = jnp.concatenate([first_half, second_half], 0)
    whole_halves = []
    for piece in (first_half, second_half):
        whole_halves.append(gather_rows(piece, splits, tensor_index))
    grad_whole = jnp.concatenate(whole_halves, 0)
    f32 = jnp.float32
    grad_cols = lax.dynamic_slice_in_dim(grad_whole, row_start, rows_dev, 2)
    left_new = beta_stat * stat_left + (1.0 - beta_stat) * jnp.einsum(
        "kij,klj->kil", grad_piece, grad_whole, preferred_element_type=f32
    )
    right_new = beta_stat * stat_right + (1.0 - beta_stat) * jnp.einsum(
        "kji,kjl->kil", grad_cols, grad_whole, preferred_element_type=f32
    )
    grad_rows = grad_piece.astype(f32)
    second_new = beta_stat * moment + (1.0 - beta_stat) * grad_rows * grad_rows
    adam_step = grad_rows / (jnp.sqrt(second_new) + eps_root)
    three_pass = lax.DotAlgorithmPreset.BF16_BF16_F32_X3
    precond_parts = []
    for part, whole in enumerate(whole_halves):
        lo = part * half
        hi = lo + whole.shape[0]
        mixed = jnp.einsum(
            "kij,kjl->kil", root_left[lo:hi], whole.astype(f32),
            precision=three_pass, preferred_element_type=f32,
        )
        precond_parts.append(jnp.einsum(
            "kij,kjl->kil", mixed, root_right[lo:hi], precision=three_pass,
            preferred_element_type=f32,
        ))
    precond = jnp.concatenate(precond_parts, 0)
    precond_sq = jnp.concatenate([jnp.sum(p * p, axis=(1, 2)) for p in precond_parts])
    sums = jnp.stack(
        [jnp.sum(adam_step * adam_step, axis=(1, 2)), precond_sq]
    )
    step = 1
    while step < splits:
        sums = sums + lax.ppermute(sums, "tensor", [(i, i ^ step) for i in range(splits)])
        step *= 2
    adam_sum, precond_sum = sums[0], sums[1]
    entries = float(rows_dev * splits * order)
    scale_ratio = jnp.sqrt(adam_sum / entries + eps_mean) / jnp.sqrt(
        precond_sum / entries + eps_mean
    )
    velocity_new = beta_mom * momentum + (1.0 - beta_mom) * scale_ratio[:, None, None] * precond
    weight_new = master - learn_rate * velocity_new
    weight_half = weight_new.astype(jnp.bfloat16)
    returning = jnp.take(weight_half, slot_of_src, axis=0, mode="clip")
    back_rows = lax.all_to_all(returning, "shard", split_axis=0, concat_axis=0, tiled=True)
    weights_local = jnp.take(back_rows, local_owner, axis=0, mode="clip")
    return (left_new, right_new, second_new, velocity_new, weight_new, weights_local)


def solution(mesh):
    placed = (
        P("shard", "tensor", None),
        P(),
        P(),
        P("shard", "tensor", None),
        P("shard", "tensor", None),
        P("shard", "tensor", None),
        P("shard", None, None),
        P("shard", "tensor", None),
        P("shard", "tensor", None),
        P("shard", "tensor", None),
    )

    return jax.shard_map(
        on_device,
        mesh=mesh,
        in_specs=placed,
        out_specs=(
            P("shard", "tensor", None),
            P("shard", "tensor", None),
            P("shard", "tensor", None),
            P("shard", "tensor", None),
            P("shard", "tensor", None),
            P("shard", "tensor", None),
        ),
        check_vma=False,
    )
```

```python
import jax
import jax.numpy as jnp
from jax import lax
from jax.sharding import PartitionSpec as P


beta_stat = 0.95
beta_mom = 0.9
learn_rate = 0.01
eps_root = 1e-08
eps_mean = 1e-06


def gather_rows(piece, far_right, splits, tensor_index):
    right = [(i, (i + 1) % splits) for i in range(splits)]
    left = [(i, (i - 1) % splits) for i in range(splits)]
    from_left = lax.ppermute(piece, "tensor", right)
    from_right = lax.ppermute(piece, "tensor", left)
    if far_right:
        far = lax.ppermute(from_left, "tensor", right)
    else:
        far = lax.ppermute(from_right, "tensor", left)
    by_shift = (piece, from_right, far, from_left)

    def ordered(first):
        return lambda: jnp.concatenate([by_shift[(p - first) % splits] for p in range(splits)], 1)

    return lax.switch(tensor_index, [ordered(first) for first in range(splits)])


def pick(source, index, valid):
    taken = jnp.take(source, index, axis=0, mode="clip")
    return jnp.where(valid[:, None, None], taken, jnp.zeros((), source.dtype))


def on_device(
    grads, owner, slot, stat_left, stat_right, root_left, root_right, moment, momentum, master
):
    groups = lax.axis_size("shard")
    splits = lax.axis_size("tensor")
    slots_dev = stat_left.shape[0]
    rows_dev = stat_left.shape[1]
    order = stat_left.shape[2]
    blocks_group = grads.shape[0]
    shard_index = lax.axis_index("shard")
    tensor_index = lax.axis_index("tensor")
    local_owner = lax.dynamic_slice_in_dim(owner, shard_index * blocks_group, blocks_group)
    slot_ids = jnp.arange(slots_dev, dtype=jnp.int32)
    group_ids = jnp.arange(groups, dtype=jnp.int32)
    owner_grid = owner.reshape(groups, blocks_group)
    slot_grid = slot.reshape(groups, blocks_group)
    hit_mask = owner_grid == shard_index
    slot_match = jnp.any(
        (slot_grid[None, :, :] == slot_ids[:, None, None]) & hit_mask[None, :, :], axis=2
    )
    src_of_slot = jnp.argmax(slot_match, axis=1).astype(jnp.int32)
    slot_filled = jnp.any(slot_match, axis=1)
    slot_of_src = jnp.argmax(slot_match, axis=0).astype(jnp.int32)
    dest_match = local_owner[None, :] == group_ids[:, None]
    block_of_dest = jnp.argmax(dest_match, axis=1).astype(jnp.int32)
    dest_used = jnp.any(dest_match, axis=1)
    row_start = tensor_index * rows_dev
    outgoing = pick(grads, block_of_dest, dest_used)
    arrived = lax.all_to_all(outgoing, "shard", split_axis=0, concat_axis=0, tiled=True)
    half = slots_dev // 2
    first_half = pick(arrived, src_of_slot[:half], slot_filled[:half])
    second_half = pick(arrived, src_of_slot[half:], slot_filled[half:])
    grad_piece = jnp.concatenate([first_half, second_half], 0)
    whole_halves = [
        gather_rows(first_half, True, splits, tensor_index),
        gather_rows(second_half, False, splits, tensor_index),
    ]
    grad_whole = jnp.concatenate(whole_halves, 0)
    f32 = jnp.float32
    grad_cols = lax.dynamic_slice_in_dim(grad_whole, row_start, rows_dev, 2)
    left_new = beta_stat * stat_left + (1.0 - beta_stat) * jnp.einsum(
        "kij,klj->kil", grad_piece, grad_whole, preferred_element_type=f32
    )
    right_new = beta_stat * stat_right + (1.0 - beta_stat) * jnp.einsum(
        "kji,kjl->kil", grad_cols, grad_whole, preferred_element_type=f32
    )
    grad_rows = grad_piece.astype(f32)
    second_new = beta_stat * moment + (1.0 - beta_stat) * grad_rows * grad_rows
    adam_step = grad_rows / (jnp.sqrt(second_new) + eps_root)
    three_pass = lax.DotAlgorithmPreset.BF16_BF16_F32_X3
    precond_parts = []
    for part, whole in enumerate(whole_halves):
        lo = part * half
        mixed = jnp.einsum(
            "kij,kjl->kil", root_left[lo : lo + half], whole.astype(f32),
            precision=three_pass, preferred_element_type=f32,
        )
        precond_parts.append(jnp.einsum(
            "kij,kjl->kil", mixed, root_right[lo : lo + half], precision=three_pass,
            preferred_element_type=f32,
        ))
    precond = jnp.concatenate(precond_parts, 0)
    precond_sq = jnp.concatenate([jnp.sum(p * p, axis=(1, 2)) for p in precond_parts])
    sums = jnp.stack(
        [jnp.sum(adam_step * adam_step, axis=(1, 2)), precond_sq]
    )
    step = 1
    while step < splits:
        sums = sums + lax.ppermute(sums, "tensor", [(i, i ^ step) for i in range(splits)])
        step *= 2
    adam_sum, precond_sum = sums[0], sums[1]
    entries = float(rows_dev * splits * order)
    scale_ratio = jnp.sqrt(adam_sum / entries + eps_mean) / jnp.sqrt(
        precond_sum / entries + eps_mean
    )
    velocity_new = beta_mom * momentum + (1.0 - beta_mom) * scale_ratio[:, None, None] * precond
    weight_new = master - learn_rate * velocity_new
    weight_half = weight_new.astype(jnp.bfloat16)
    returning = jnp.take(weight_half, slot_of_src, axis=0, mode="clip")
    back_rows = lax.all_to_all(returning, "shard", split_axis=0, concat_axis=0, tiled=True)
    weights_local = jnp.take(back_rows, local_owner, axis=0, mode="clip")
    return (left_new, right_new, second_new, velocity_new, weight_new, weights_local)


def solution(mesh):
    placed = (
        P("shard", "tensor", None),
        P(),
        P(),
        P("shard", "tensor", None),
        P("shard", "tensor", None),
        P("shard", "tensor", None),
        P("shard", None, None),
        P("shard", "tensor", None),
        P("shard", "tensor", None),
        P("shard", "tensor", None),
    )

    return jax.shard_map(
        on_device,
        mesh=mesh,
        in_specs=placed,
        out_specs=(
            P("shard", "tensor", None),
            P("shard", "tensor", None),
            P("shard", "tensor", None),
            P("shard", "tensor", None),
            P("shard", "tensor", None),
            P("shard", "tensor", None),
        ),
        check_vma=False,
    )
```

```python
import jax
import jax.numpy as jnp
from jax import lax
from jax.sharding import PartitionSpec as P


beta_stat = 0.95
beta_mom = 0.9
learn_rate = 0.01
eps_root = 1e-08
eps_mean = 1e-06


def gather_rows(piece, far_right, splits, tensor_index):
    right = [(i, (i + 1) % splits) for i in range(splits)]
    left = [(i, (i - 1) % splits) for i in range(splits)]
    from_left = lax.ppermute(piece, "tensor", right)
    from_right = lax.ppermute(piece, "tensor", left)
    if far_right:
        far = lax.ppermute(from_left, "tensor", right)
    else:
        far = lax.ppermute(from_right, "tensor", left)
    by_shift = (piece, from_right, far, from_left)

    def ordered(first):
        return lambda: jnp.concatenate([by_shift[(p - first) % splits] for p in range(splits)], 1)

    return lax.switch(tensor_index, [ordered(first) for first in range(splits)])


def pick(source, index, valid):
    taken = jnp.take(source, index, axis=0, mode="clip")
    return jnp.where(valid[:, None, None], taken, jnp.zeros((), source.dtype))


def on_device(
    grads, owner, slot, stat_left, stat_right, root_left, root_right, moment, momentum, master
):
    groups = lax.axis_size("shard")
    splits = lax.axis_size("tensor")
    slots_dev = stat_left.shape[0]
    rows_dev = stat_left.shape[1]
    order = stat_left.shape[2]
    blocks_group = grads.shape[0]
    shard_index = lax.axis_index("shard")
    tensor_index = lax.axis_index("tensor")
    owner_grid = owner.reshape(groups, blocks_group)
    slot_grid = slot.reshape(groups, blocks_group)
    local_owner = lax.dynamic_index_in_dim(owner_grid, shard_index, 0, keepdims=False)
    hit_mask = owner_grid == shard_index
    slot_ids = jnp.arange(slots_dev, dtype=jnp.int32)
    group_ids = jnp.arange(groups, dtype=jnp.int32)
    slot_match = jnp.any(
        (slot_grid[None, :, :] == slot_ids[:, None, None]) & hit_mask[None, :, :], axis=2
    )
    src_of_slot = jnp.argmax(slot_match, axis=1).astype(jnp.int32)
    slot_filled = jnp.any(slot_match, axis=1)
    slot_of_src = jnp.argmax(slot_match, axis=0).astype(jnp.int32)
    dest_match = local_owner[None, :] == group_ids[:, None]
    block_of_dest = jnp.argmax(dest_match, axis=1).astype(jnp.int32)
    dest_used = jnp.any(dest_match, axis=1)
    row_start = tensor_index * rows_dev
    outgoing = pick(grads, block_of_dest, dest_used)
    arrived = lax.all_to_all(outgoing, "shard", split_axis=0, concat_axis=0, tiled=True)
    half = slots_dev // 2
    first_half = pick(arrived, src_of_slot[:half], slot_filled[:half])
    second_half = pick(arrived, src_of_slot[half:], slot_filled[half:])
    grad_piece = jnp.concatenate([first_half, second_half], 0)
    whole_halves = [
        gather_rows(first_half, True, splits, tensor_index),
        gather_rows(second_half, False, splits, tensor_index),
    ]
    grad_whole = jnp.concatenate(whole_halves, 0)
    f32 = jnp.float32
    grad_cols = lax.dynamic_slice_in_dim(grad_whole, row_start, rows_dev, 2)
    left_new = beta_stat * stat_left + (1.0 - beta_stat) * jnp.einsum(
        "kij,klj->kil", grad_piece, grad_whole, preferred_element_type=f32
    )
    right_new = beta_stat * stat_right + (1.0 - beta_stat) * jnp.einsum(
        "kji,kjl->kil", grad_cols, grad_whole, preferred_element_type=f32
    )
    grad_rows = grad_piece.astype(f32)
    second_new = beta_stat * moment + (1.0 - beta_stat) * grad_rows * grad_rows
    adam_step = grad_rows / (jnp.sqrt(second_new) + eps_root)
    three_pass = lax.DotAlgorithmPreset.BF16_BF16_F32_X3
    precond_parts = []
    for part, whole in enumerate(whole_halves):
        lo = part * half
        mixed = jnp.einsum(
            "kij,kjl->kil", root_left[lo : lo + half], whole.astype(f32),
            precision=three_pass, preferred_element_type=f32,
        )
        precond_parts.append(jnp.einsum(
            "kij,kjl->kil", mixed, root_right[lo : lo + half], precision=three_pass,
            preferred_element_type=f32,
        ))
    precond = jnp.concatenate(precond_parts, 0)
    precond_sq = jnp.concatenate([jnp.sum(p * p, axis=(1, 2)) for p in precond_parts])
    sums = jnp.stack(
        [jnp.sum(adam_step * adam_step, axis=(1, 2)), precond_sq]
    )
    step = 1
    while step < splits:
        sums = sums + lax.ppermute(sums, "tensor", [(i, i ^ step) for i in range(splits)])
        step *= 2
    adam_sum, precond_sum = sums[0], sums[1]
    entries = float(rows_dev * splits * order)
    scale_ratio = jnp.sqrt(adam_sum / entries + eps_mean) / jnp.sqrt(
        precond_sum / entries + eps_mean
    )
    velocity_soon = beta_mom * momentum + (1.0 - beta_mom) * scale_ratio[:, None, None] * precond
    weight_half = (master - learn_rate * velocity_soon).astype(jnp.bfloat16)
    held = lax.optimization_barrier((momentum, master, precond, scale_ratio, weight_half))
    velocity_new = beta_mom * held[0] + (1.0 - beta_mom) * held[3][:, None, None] * held[2]
    weight_new = held[1] - learn_rate * velocity_new
    weight_half = held[4]
    returning = jnp.take(weight_half, slot_of_src, axis=0, mode="clip")
    back_rows = lax.all_to_all(returning, "shard", split_axis=0, concat_axis=0, tiled=True)
    weights_local = jnp.take(back_rows, local_owner, axis=0, mode="clip")
    return (left_new, right_new, second_new, velocity_new, weight_new, weights_local)


def solution(mesh):
    placed = (
        P("shard", "tensor", None),
        P(),
        P(),
        P("shard", "tensor", None),
        P("shard", "tensor", None),
        P("shard", "tensor", None),
        P("shard", None, None),
        P("shard", "tensor", None),
        P("shard", "tensor", None),
        P("shard", "tensor", None),
    )

    return jax.shard_map(
        on_device,
        mesh=mesh,
        in_specs=placed,
        out_specs=(
            P("shard", "tensor", None),
            P("shard", "tensor", None),
            P("shard", "tensor", None),
            P("shard", "tensor", None),
            P("shard", "tensor", None),
            P("shard", "tensor", None),
        ),
        check_vma=False,
    )
```

```python
import jax
import jax.numpy as jnp
from jax import lax
from jax.sharding import PartitionSpec as P


beta_stat = 0.95
beta_mom = 0.9
learn_rate = 0.01
eps_root = 1e-08
eps_mean = 1e-06


def gather_rows(piece, far_right, splits, tensor_index):
    right = [(i, (i + 1) % splits) for i in range(splits)]
    left = [(i, (i - 1) % splits) for i in range(splits)]
    from_left = lax.ppermute(piece, "tensor", right)
    from_right = lax.ppermute(piece, "tensor", left)
    if far_right:
        far = lax.ppermute(from_left, "tensor", right)
    else:
        far = lax.ppermute(from_right, "tensor", left)
    by_shift = (piece, from_right, far, from_left)

    def ordered(first):
        return lambda: jnp.concatenate([by_shift[(p - first) % splits] for p in range(splits)], 1)

    return lax.switch(tensor_index, [ordered(first) for first in range(splits)])


def pick(source, index, valid):
    taken = jnp.take(source, index, axis=0, mode="clip")
    return jnp.where(valid[:, None, None], taken, jnp.zeros((), source.dtype))


def on_device(
    grads, owner, slot, stat_left, stat_right, root_left, root_right, moment, momentum, master
):
    groups = lax.axis_size("shard")
    splits = lax.axis_size("tensor")
    slots_dev = stat_left.shape[0]
    rows_dev = stat_left.shape[1]
    order = stat_left.shape[2]
    blocks_group = grads.shape[0]
    shard_index = lax.axis_index("shard")
    tensor_index = lax.axis_index("tensor")
    owner_grid = owner.reshape(groups, blocks_group)
    slot_grid = slot.reshape(groups, blocks_group)
    local_owner = lax.dynamic_index_in_dim(owner_grid, shard_index, 0, keepdims=False)
    hit_mask = owner_grid == shard_index
    slot_ids = jnp.arange(slots_dev, dtype=jnp.int32)
    group_ids = jnp.arange(groups, dtype=jnp.int32)
    slot_match = jnp.any(
        (slot_grid[None, :, :] == slot_ids[:, None, None]) & hit_mask[None, :, :], axis=2
    )
    src_of_slot = jnp.argmax(slot_match, axis=1).astype(jnp.int32)
    slot_filled = jnp.any(slot_match, axis=1)
    slot_of_src = jnp.argmax(slot_match, axis=0).astype(jnp.int32)
    dest_match = local_owner[None, :] == group_ids[:, None]
    block_of_dest = jnp.argmax(dest_match, axis=1).astype(jnp.int32)
    dest_used = jnp.any(dest_match, axis=1)
    row_start = tensor_index * rows_dev
    outgoing = pick(grads, block_of_dest, dest_used)
    arrived = lax.all_to_all(outgoing, "shard", split_axis=0, concat_axis=0, tiled=True)
    half = slots_dev // 2
    first_half = pick(arrived, src_of_slot[:half], slot_filled[:half])
    second_half = pick(arrived, src_of_slot[half:], slot_filled[half:])
    grad_piece = jnp.concatenate([first_half, second_half], 0)
    whole_halves = [
        gather_rows(first_half, True, splits, tensor_index),
        gather_rows(second_half, False, splits, tensor_index),
    ]
    grad_whole = jnp.concatenate(whole_halves, 0)
    f32 = jnp.float32
    grad_cols = lax.dynamic_slice_in_dim(grad_whole, row_start, rows_dev, 2)
    left_new = beta_stat * stat_left + (1.0 - beta_stat) * jnp.einsum(
        "kij,klj->kil", grad_piece, grad_whole, preferred_element_type=f32
    )
    right_new = beta_stat * stat_right + (1.0 - beta_stat) * jnp.einsum(
        "kji,kjl->kil", grad_cols, grad_whole, preferred_element_type=f32
    )
    grad_rows = grad_piece.astype(f32)
    second_new = beta_stat * moment + (1.0 - beta_stat) * grad_rows * grad_rows
    adam_step = grad_rows / (jnp.sqrt(second_new) + eps_root)
    three_pass = lax.DotAlgorithmPreset.BF16_BF16_F32_X3
    precond_parts = []
    for part, whole in enumerate(whole_halves):
        lo = part * half
        mixed = jnp.einsum(
            "kij,kjl->kil", root_left[lo : lo + half], whole.astype(f32),
            precision=three_pass, preferred_element_type=f32,
        )
        precond_parts.append(jnp.einsum(
            "kij,kjl->kil", mixed, root_right[lo : lo + half], precision=three_pass,
            preferred_element_type=f32,
        ))
    precond = jnp.concatenate(precond_parts, 0)
    precond_sq = jnp.concatenate([jnp.sum(p * p, axis=(1, 2)) for p in precond_parts])
    sums = jnp.stack(
        [jnp.sum(adam_step * adam_step, axis=(1, 2)), precond_sq]
    )
    step = splits // 2
    while step >= 1:
        sums = sums + lax.ppermute(sums, "tensor", [(i, i ^ step) for i in range(splits)])
        step //= 2
    adam_sum, precond_sum = sums[0], sums[1]
    entries = float(rows_dev * splits * order)
    scale_ratio = jnp.sqrt(adam_sum / entries + eps_mean) / jnp.sqrt(
        precond_sum / entries + eps_mean
    )
    velocity_new = beta_mom * momentum + (1.0 - beta_mom) * scale_ratio[:, None, None] * precond
    weight_new = master - learn_rate * velocity_new
    weight_half = weight_new.astype(jnp.bfloat16)
    returning = jnp.take(weight_half, slot_of_src, axis=0, mode="clip")
    back_rows = lax.all_to_all(returning, "shard", split_axis=0, concat_axis=0, tiled=True)
    weights_local = jnp.take(back_rows, local_owner, axis=0, mode="clip")
    return (left_new, right_new, second_new, velocity_new, weight_new, weights_local)


def solution(mesh):
    placed = (
        P("shard", "tensor", None),
        P(),
        P(),
        P("shard", "tensor", None),
        P("shard", "tensor", None),
        P("shard", "tensor", None),
        P("shard", None, None),
        P("shard", "tensor", None),
        P("shard", "tensor", None),
        P("shard", "tensor", None),
    )

    return jax.shard_map(
        on_device,
        mesh=mesh,
        in_specs=placed,
        out_specs=(
            P("shard", "tensor", None),
            P("shard", "tensor", None),
            P("shard", "tensor", None),
            P("shard", "tensor", None),
            P("shard", "tensor", None),
            P("shard", "tensor", None),
        ),
        check_vma=False,
    )
```
